128 devices in a mesh: pts: 128 (over y, x, z, core).
Axes of the slice: x: 4, y: 4, z: 4, core: 2. Of those that a mesh axis runs over, the one named last changes fastest.
Arguments:
- inputs: bfloat16 [131072, 128], P('pts'), may hold values from -6 to 6
- targets: float32 [131072], P('pts'), may hold values from -6 to 6
- skeletons: int32 [127, 256], replicated, may hold values from 0 to 131071, as said below
- w_in: bfloat16 [128, 1024], replicated, may hold values from -0.5 to 0.5
- w_mid: bfloat16 [1024, 1024], replicated, may hold values from -0.1875 to 0.1875
- w_out: bfloat16 [8, 1024], replicated, may hold values from -0.1875 to 0.1875
Outputs:
- solution: float32 [131072], P('pts')
- grad_in: float32 [128, 1024], replicated
- grad_mid: float32 [1024, 1024], replicated
- grad_out: float32 [8, 1024], replicated
The draws below stay inside these ranges and needn't reach their ends.
Inputs may be any that keep to these rules, and one draw needn't show every extreme that they name: `skeletons`: row c - 1 belongs to inner node c. Its first 128 entries lie in the left half of C_c, its last 128 in the right half; each half is cut into 128 equal consecutive buckets and entry j lies in bucket j, so the entries rise; the first entry is the left half's first point and the last entry the right half's last point.
All inputs are finite; a program needn't handle non-finite values.
Results may differ from the reference program's by a relative error of at most 0.0087.
Values sent between devices are 32-bit elements; how exact they have to be, the bound alone decides.
No kernel may reach another device: no remote copies, remote signals or barrier semaphores. Data moves between devices by JAX's collectives and lax.ppermute only.
A program may use at most 128 MiB of HBM per device.

```python
import math
import jax
import jax.numpy as jnp
from jax import lax

LEAF = 1024
RANK = 128
DIN = 128
HID = 1024
FEAT = 8
ITERS = 2
POINTS = 131072
N_PTS = 128


def draw_skeletons(key, part):
    levels = N_PTS.bit_length() - 1
    node_ids = jnp.arange(1, N_PTS, dtype=jnp.int32)
    depth_node = jnp.zeros_like(node_ids)
    for height in range(1, levels):
        depth_node = depth_node + (node_ids >= 1 << height).astype(jnp.int32)
    span_dev = jnp.right_shift(jnp.int32(N_PTS), depth_node)
    start_dev = (node_ids - jnp.left_shift(jnp.int32(1), depth_node)) * span_dev
    half_points = span_dev // 2 * LEAF
    stride = half_points // RANK
    bucket = jnp.arange(RANK, dtype=jnp.int32)
    offsets = jax.random.randint(key, (N_PTS - 1, 2, RANK), 0, 1 << 30, dtype=jnp.int32) % stride[:, None, None]
    offsets = offsets.at[:, 0, 0].set(0)
    offsets = offsets.at[:, 1, RANK - 1].set(stride - 1)
    base_index = start_dev[:, None] * LEAF + bucket[None, :] * stride[:, None]
    left_half = base_index + offsets[:, 0]
    right_half = base_index + half_points[:, None] + offsets[:, 1]
    return jnp.concatenate([left_half, right_half], axis=1).astype(jnp.int32)


def level_of(rng, extent, cuts, least, top_value):
    gain = 1.0
    for dim, blocks in cuts:
        steps = jax.random.uniform(jax.random.fold_in(jax.random.fold_in(rng, 6), dim), (blocks,), jnp.float32, least / len(cuts), top_value / len(cuts))
        gain = gain * jnp.repeat(jnp.exp(steps), extent[dim] // blocks).reshape((-1,) + (1,) * (len(extent) - 1 - dim))
    return gain


def centred(stream_key, shape, spread, most, split=(), held_as=jnp.bfloat16):
    factor_of = level_of(stream_key, shape, split, -0.22, 0.18) if split else 1.0
    values = jax.random.normal(stream_key, shape, jnp.float32) * spread * factor_of
    return jnp.minimum(jnp.maximum(values, -most), most).astype(held_as)


def setup_inputs(seed: int = 0) -> dict:
    seeds = jax.random.split(jax.random.key(seed), 7)
    inputs = centred(seeds[0], (POINTS, DIN), 1.0, 6.0, ((0, 128),))
    targets = centred(seeds[1], (POINTS,), 1.0, 6.0, ((0, 128),), jnp.float32)
    skeletons = draw_skeletons(jax.random.fold_in(seeds[6], 71), 0)
    w_in = centred(seeds[3], (DIN, HID), DIN ** -0.5, 0.5)
    w_mid = centred(seeds[4], (HID, HID), HID ** -0.5, 0.1875)
    w_out = centred(seeds[5], (FEAT, HID), HID ** -0.5, 0.1875)
    return {"inputs": inputs, "targets": targets, "skeletons": skeletons, "w_in": w_in, "w_mid": w_mid, "w_out": w_out}


noise_level = 1.0
highest = lax.Precision.HIGHEST

def kernel_block(left_feats, right_feats):
    cross_term = jnp.dot(left_feats.T, right_feats, precision=highest, preferred_element_type=jnp.float32)
    norm_left = lax.optimization_barrier(jnp.sum(left_feats * left_feats, axis=0))
    norm_right = lax.optimization_barrier(jnp.sum(right_feats * right_feats, axis=0))
    return jnp.exp(-0.5 * (norm_left[:, None] + norm_right[None, :] - 2.0 * cross_term))

def silu_slope(pre_act):
    sigmoid_val = jax.nn.sigmoid(pre_act)
    return sigmoid_val * (1.0 + pre_act * (1.0 - sigmoid_val))

def forward(inputs, w_in, w_mid, w_out):
    pre_one = jnp.dot(inputs, w_in, preferred_element_type=jnp.float32)
    hid_one = jax.nn.silu(pre_one).astype(jnp.bfloat16)
    pre_two = jnp.dot(hid_one, w_mid, preferred_element_type=jnp.float32)
    hid_two = jax.nn.silu(pre_two).astype(jnp.bfloat16)
    features = lax.dot_general(w_out, hid_two, (((1,), (1,)), ((), ())), preferred_element_type=jnp.float32)
    return (pre_one, hid_one, pre_two, hid_two, features)

def backward(inputs, w_mid, w_out, pre_one, hid_one, pre_two, hid_two, feat_grad):
    low_grad = feat_grad.astype(jnp.bfloat16)
    grad_out = jnp.dot(low_grad, hid_two, preferred_element_type=jnp.float32)
    back_two = lax.dot_general(low_grad, w_out, (((0,), (0,)), ((), ())), preferred_element_type=jnp.float32)
    grad_two = (back_two * silu_slope(pre_two)).astype(jnp.bfloat16)
    grad_mid = lax.dot_general(hid_one, grad_two, (((0,), (0,)), ((), ())), preferred_element_type=jnp.float32)
    back_one = lax.dot_general(grad_two, w_mid, (((1,), (1,)), ((), ())), preferred_element_type=jnp.float32)
    grad_one = (back_one * silu_slope(pre_one)).astype(jnp.bfloat16)
    grad_in = lax.dot_general(inputs, grad_one, (((0,), (0,)), ((), ())), preferred_element_type=jnp.float32)
    return (grad_in, grad_mid, grad_out)

def device_blocks(features):
    return jnp.transpose(features.reshape(FEAT, N_PTS, LEAF), (1, 0, 2))

def level_skeletons(features, skeletons, height):
    group_size = 2 ** (height + 1)
    skel_rows = skeletons[(N_PTS >> height + 1) - 1:(N_PTS >> height) - 1]
    chosen = jnp.transpose(features[:, skel_rows], (1, 0, 2))
    return (jnp.repeat(chosen, group_size, axis=0), group_size)

def project(blocks, skel_feats, vec_blocks):

    def one_block(parts):
        return jnp.dot(parts[2], kernel_block(parts[0], parts[1]), precision=highest, preferred_element_type=jnp.float32)
    return lax.map(jax.checkpoint(one_block), (blocks, skel_feats, vec_blocks))

def expand(blocks, skel_feats, node_vals):

    def one_block(parts):
        return jnp.dot(kernel_block(parts[0], parts[1]), parts[2], precision=highest, preferred_element_type=jnp.float32)
    return lax.map(one_block, (blocks, skel_feats, node_vals))

def node_sums(local_part, group_size):
    return lax.optimization_barrier(jnp.sum(local_part.reshape(-1, group_size, local_part.shape[-1]), axis=1))

def leaf_apply(blocks, vec_blocks):

    def one_block(parts):
        return jnp.dot(kernel_block(parts[0], parts[0]), parts[1], precision=highest, preferred_element_type=jnp.float32)
    return lax.map(one_block, (blocks, vec_blocks))

def apply_operator(vector, features, skeletons):
    levels = N_PTS.bit_length() - 1
    blocks = device_blocks(features)
    vec_blocks = vector.reshape(N_PTS, LEAF)
    running = noise_level * vec_blocks + leaf_apply(blocks, vec_blocks)
    for height in range(levels):
        skel_feats, group_size = level_skeletons(features, skeletons, height)
        sums_here = node_sums(project(blocks, skel_feats, vec_blocks), group_size)
        running = running + expand(blocks, skel_feats, jnp.repeat(sums_here, group_size, axis=0)) / (2 * RANK)
    return running.reshape(-1)

def quadratic(features, solution, skeletons):
    levels = N_PTS.bit_length() - 1
    blocks = device_blocks(features)
    vec_blocks = solution.reshape(N_PTS, LEAF)

    def leaf_value(parts):
        return 0.5 * jnp.dot(parts[1], jnp.dot(kernel_block(parts[0], parts[0]), parts[1], precision=highest, preferred_element_type=jnp.float32), precision=highest)
    quad_value = 0.5 * noise_level * jnp.sum(solution * solution)
    quad_value = quad_value + jnp.sum(lax.map(jax.checkpoint(leaf_value), (blocks, vec_blocks)))
    for height in range(levels):
        skel_feats, group_size = level_skeletons(features, skeletons, height)
        sums_here = node_sums(project(blocks, skel_feats, vec_blocks), group_size)
        quad_value = quad_value + jnp.sum(sums_here * sums_here) / (4 * RANK)
    return quad_value / math.sqrt(POINTS)

def reference(inputs, targets, skeletons, w_in, w_mid, w_out):
    pre_one, hid_one, pre_two, hid_two, features = forward(inputs, w_in, w_mid, w_out)
    solution = jnp.zeros_like(targets)
    residual = targets
    direction = targets
    res_norm = jnp.sum(residual * residual)
    for iteration in range(ITERS):
        image_vec = apply_operator(direction, features, skeletons)
        step_size = res_norm / jnp.sum(direction * image_vec)
        solution = solution + step_size * direction
        if iteration + 1 < ITERS:
            residual = residual - step_size * image_vec
            new_norm = jnp.sum(residual * residual)
            direction = residual + new_norm / res_norm * direction
            res_norm = new_norm
    feat_grad = jax.grad(quadratic)(features, solution, skeletons)
    grad_in, grad_mid, grad_out = backward(inputs, w_mid, w_out, pre_one, hid_one, pre_two, hid_two, feat_grad)
    return (solution, grad_in, grad_mid, grad_out)
```

```python
import math

import jax
import jax.numpy as jnp
from jax import lax
from jax.sharding import PartitionSpec as P

ITERS = 2


noise_level = 1.0
highest = lax.Precision.HIGHEST


def kernel_block(left_feats, right_feats):
    cross_term = jnp.dot(
        left_feats.T, right_feats, precision=highest, preferred_element_type=jnp.float32
    )
    norm_left = jnp.sum(left_feats * left_feats, axis=0)
    norm_right = jnp.sum(right_feats * right_feats, axis=0)
    return jnp.exp(-0.5 * (norm_left[:, None] + norm_right[None, :] - 2.0 * cross_term))


def silu_slope(pre_act):
    sigmoid_val = jax.nn.sigmoid(pre_act)
    return sigmoid_val * (1.0 + pre_act * (1.0 - sigmoid_val))


def butterfly(parts, scalars, bits, devices, hook=None):
    parts = list(parts)
    for b in range(bits):
        live = [p.reshape(-1) for p in parts[b:]]
        if scalars is not None:
            live.append(scalars)
        payload = jnp.concatenate(live) if len(live) > 1 else live[0]
        recv = lax.ppermute(payload, "pts", [(i, i ^ (1 << b)) for i in range(devices)])
        total = payload + recv
        offset = 0
        for h in range(b, len(parts)):
            size = parts[h].size
            parts[h] = total[offset:offset + size].reshape(parts[h].shape)
            offset += size
        if scalars is not None:
            scalars = total[offset:]
        if hook is not None:
            scalars = hook(b, parts[b], scalars)
    return parts, scalars


def on_device(inputs, targets, skeletons, w_in, w_mid, w_out):
    devices = lax.axis_size("pts")
    levels = devices.bit_length() - 1
    device_id = lax.axis_index("pts")
    leaf_size = inputs.shape[0]
    skel_width = skeletons.shape[1]
    points = leaf_size * devices
    pre_one = jnp.dot(inputs, w_in, preferred_element_type=jnp.float32)
    hid_one = jax.nn.silu(pre_one).astype(jnp.bfloat16)
    pre_two = jnp.dot(hid_one, w_mid, preferred_element_type=jnp.float32)
    hid_two = jax.nn.silu(pre_two).astype(jnp.bfloat16)
    features = lax.dot_general(
        w_out, hid_two, (((1,), (1,)), ((), ())), preferred_element_type=jnp.float32
    )

    rows = jnp.stack(
        [
            lax.dynamic_index_in_dim(
                skeletons, jnp.right_shift(devices + device_id, height + 1) - 1, 0, False
            )
            for height in range(levels)
        ]
    )
    local_slots = rows - device_id * leaf_size
    route = (local_slots[:, :, None] == jnp.arange(leaf_size)[None, None, :]).astype(jnp.float32)
    pieces = jnp.einsum("fp,lsp->lfs", features, route, precision=highest)

    res_local = jnp.sum(targets * targets)
    skel_parts, scal = butterfly(list(pieces), res_local[None], levels, devices)
    res_norm = scal[0]
    skel_feats = jnp.stack(skel_parts)

    leaf_kernel = kernel_block(features, features)
    basis_maps = jnp.stack([kernel_block(features, skel_feats[h]) for h in range(levels)])

    def node_term(height, part, scalars):
        return scalars + jnp.concatenate(
            [jnp.zeros((1,), jnp.float32), (jnp.sum(part * part) / skel_width)[None]]
        )

    dir0 = targets
    near0 = jnp.dot(leaf_kernel, dir0, precision=highest, preferred_element_type=jnp.float32)
    proj0 = jnp.einsum("lps,p->ls", basis_maps, dir0, precision=highest)
    own0 = jnp.sum(dir0 * (noise_level * dir0 + near0))
    parts0, scal0 = butterfly(
        list(proj0), jnp.stack([own0, jnp.zeros((), jnp.float32)]), levels, devices, node_term
    )
    node0 = jnp.stack(parts0)
    curve0 = scal0[0] + scal0[1]
    step0 = res_norm / curve0
    far0 = jnp.einsum("lps,ls->p", basis_maps, node0, precision=highest) / skel_width
    image0 = noise_level * dir0 + near0 + far0
    sol_half = step0 * dir0
    resid = dir0 - step0 * image0

    near_res = jnp.dot(leaf_kernel, resid, precision=highest, preferred_element_type=jnp.float32)
    proj_res = jnp.einsum("lps,p->ls", basis_maps, resid, precision=highest)
    parts_r, scal_r = butterfly(list(proj_res), jnp.sum(resid * resid)[None], levels, devices)
    node_res = jnp.stack(parts_r)
    new_norm = scal_r[0]
    beta = new_norm / res_norm
    dir1 = resid + beta * dir0
    node1 = node_res + beta * node0
    near1 = near_res + beta * near0
    shares = jnp.sum(
        jnp.sum(node1 * node1, axis=1)
        / (skel_width * (2.0 ** jnp.arange(1, levels + 1, dtype=jnp.float32)))
    )
    own1 = jnp.sum(dir1 * (noise_level * dir1 + near1)) + shares
    _, scal1 = butterfly([], own1[None], levels, devices)
    curve1 = scal1[0]
    step1 = new_norm / curve1
    solution = sol_half + step1 * dir1
    node_sol = step0 * node0 + step1 * node1

    scaled = features * solution[None, :]
    kern_sol = jnp.dot(leaf_kernel, solution, precision=highest, preferred_element_type=jnp.float32)
    grad_leaf = solution[None, :] * (
        jnp.dot(scaled, leaf_kernel, precision=highest, preferred_element_type=jnp.float32)
        - features * kern_sol[None, :]
    )
    expand = jnp.einsum("lps,ls->p", basis_maps, node_sol, precision=highest)
    weighted = skel_feats * node_sol[:, None, :]
    pulled = jnp.einsum("lfs,lps->fp", weighted, basis_maps, precision=highest)
    grad_pts = solution[None, :] * (pulled - features * expand[None, :]) / skel_width
    toward = jnp.einsum("fp,lps->lfs", scaled, basis_maps, precision=highest)
    proj_sol = jnp.einsum("p,lps->ls", solution, basis_maps, precision=highest)
    grad_skel = node_sol[:, None, :] * (toward - skel_feats * proj_sol[:, None, :]) / skel_width
    skel_sum, _ = butterfly(list(grad_skel), None, levels, devices)
    routed = jnp.einsum("lfs,lsp->fp", jnp.stack(skel_sum), route, precision=highest)
    feat_grad = (grad_leaf + grad_pts + routed) / math.sqrt(points)

    low_grad = feat_grad.astype(jnp.bfloat16)
    grad_out = jnp.dot(low_grad, hid_two, preferred_element_type=jnp.float32)
    back_two = lax.dot_general(
        low_grad, w_out, (((0,), (0,)), ((), ())), preferred_element_type=jnp.float32
    )
    grad_two = (back_two * silu_slope(pre_two)).astype(jnp.bfloat16)
    grad_mid = lax.dot_general(
        hid_one, grad_two, (((0,), (0,)), ((), ())), preferred_element_type=jnp.float32
    )
    back_one = lax.dot_general(
        grad_two, w_mid, (((1,), (1,)), ((), ())), preferred_element_type=jnp.float32
    )
    grad_one = (back_one * silu_slope(pre_one)).astype(jnp.bfloat16)
    grad_in = lax.dot_general(
        inputs, grad_one, (((0,), (0,)), ((), ())), preferred_element_type=jnp.float32
    )
    grad_in, grad_mid, grad_out = lax.psum((grad_in, grad_mid, grad_out), "pts")
    return (solution, grad_in, grad_mid, grad_out)


def solution(mesh):
    in_specs = (P("pts", None), P("pts"), P(), P(), P(), P())
    out_specs = (P("pts"), P(), P(), P())
    return jax.shard_map(
        on_device, mesh=mesh, in_specs=in_specs, out_specs=out_specs, check_vma=False
    )
```

```python
import math

import jax
import jax.numpy as jnp
from jax import lax
from jax.sharding import PartitionSpec as P

ITERS = 2


noise_level = 1.0
highest = lax.Precision.HIGHEST


def kernel_block(left_feats, right_feats):
    cross_term = jnp.dot(
        left_feats.T, right_feats, precision=highest, preferred_element_type=jnp.float32
    )
    norm_left = jnp.sum(left_feats * left_feats, axis=0)
    norm_right = jnp.sum(right_feats * right_feats, axis=0)
    return jnp.exp(-0.5 * (norm_left[:, None] + norm_right[None, :] - 2.0 * cross_term))


def silu_slope(pre_act):
    sigmoid_val = jax.nn.sigmoid(pre_act)
    return sigmoid_val * (1.0 + pre_act * (1.0 - sigmoid_val))


def butterfly(parts, scalars, bits, devices, hook=None):
    parts = list(parts)
    for b in range(bits):
        live = [p.reshape(-1) for p in parts[b:]]
        if scalars is not None:
            live.append(scalars)
        payload = jnp.concatenate(live) if len(live) > 1 else live[0]
        recv = lax.ppermute(payload, "pts", [(i, i ^ (1 << b)) for i in range(devices)])
        total = payload + recv
        offset = 0
        for h in range(b, len(parts)):
            size = parts[h].size
            parts[h] = total[offset:offset + size].reshape(parts[h].shape)
            offset += size
        if scalars is not None:
            scalars = total[offset:]
        if hook is not None:
            scalars = hook(b, parts[b], scalars)
    return parts, scalars


def on_device(inputs, targets, skeletons, w_in, w_mid, w_out):
    devices = lax.axis_size("pts")
    levels = devices.bit_length() - 1
    device_id = lax.axis_index("pts")
    leaf_size = inputs.shape[0]
    skel_width = skeletons.shape[1]
    points = leaf_size * devices
    pre_one = jnp.dot(inputs, w_in, preferred_element_type=jnp.float32)
    hid_one = jax.nn.silu(pre_one).astype(jnp.bfloat16)
    pre_two = jnp.dot(hid_one, w_mid, preferred_element_type=jnp.float32)
    hid_two = jax.nn.silu(pre_two).astype(jnp.bfloat16)
    features = lax.dot_general(
        w_out, hid_two, (((1,), (1,)), ((), ())), preferred_element_type=jnp.float32
    )

    rows = jnp.stack(
        [
            lax.dynamic_index_in_dim(
                skeletons, jnp.right_shift(devices + device_id, height + 1) - 1, 0, False
            )
            for height in range(levels)
        ]
    )
    local_slots = rows - device_id * leaf_size
    route = (local_slots[:, :, None] == jnp.arange(leaf_size)[None, None, :]).astype(jnp.float32)
    pieces = jnp.einsum("fp,lsp->lfs", features, route, precision=highest)

    res_local = jnp.sum(targets * targets)
    skel_parts, scal = butterfly(list(pieces), res_local[None], levels, devices)
    res_norm = scal[0]
    skel_feats = jnp.stack(skel_parts)

    leaf_kernel = kernel_block(features, features)
    basis_maps = jnp.stack([kernel_block(features, skel_feats[h]) for h in range(levels)])

    def node_term(height, part, scalars):
        return scalars + jnp.concatenate(
            [jnp.zeros((1,), jnp.float32), (jnp.sum(part * part) / skel_width)[None]]
        )

    dir0 = targets
    near0 = jnp.dot(leaf_kernel, dir0, precision=highest, preferred_element_type=jnp.float32)
    proj0 = jnp.einsum("lps,p->ls", basis_maps, dir0, precision=highest)
    own0 = jnp.sum(dir0 * (noise_level * dir0 + near0))
    parts0, scal0 = butterfly(
        list(proj0), jnp.stack([own0, jnp.zeros((), jnp.float32)]), levels, devices, node_term
    )
    node0 = jnp.stack(parts0)
    curve0 = scal0[0] + scal0[1]
    step0 = res_norm / curve0
    far0 = jnp.einsum("lps,ls->p", basis_maps, node0, precision=highest) / skel_width
    image0 = noise_level * dir0 + near0 + far0
    sol_half = step0 * dir0
    resid = dir0 - step0 * image0

    near_res = jnp.dot(leaf_kernel, resid, precision=highest, preferred_element_type=jnp.float32)
    proj_res = jnp.einsum("lps,p->ls", basis_maps, resid, precision=highest)
    parts_r, scal_r = butterfly(list(proj_res), jnp.sum(resid * resid)[None], levels, devices)
    node_res = jnp.stack(parts_r)
    new_norm = scal_r[0]
    beta = new_norm / res_norm
    dir1 = resid + beta * dir0
    node1 = node_res + beta * node0
    near1 = near_res + beta * near0
    shares = jnp.sum(
        jnp.sum(node1 * node1, axis=1)
        / (skel_width * (2.0 ** jnp.arange(1, levels + 1, dtype=jnp.float32)))
    )
    own1 = jnp.sum(dir1 * (noise_level * dir1 + near1)) + shares
    _, scal1 = butterfly([], own1[None], levels, devices)
    curve1 = scal1[0]
    step1 = new_norm / curve1
    solution = sol_half + step1 * dir1
    node_sol = step0 * node0 + step1 * node1

    scaled = features * solution[None, :]
    kern_sol = jnp.dot(leaf_kernel, solution, precision=highest, preferred_element_type=jnp.float32)
    grad_leaf = solution[None, :] * (
        jnp.dot(scaled, leaf_kernel, precision=highest, preferred_element_type=jnp.float32)
        - features * kern_sol[None, :]
    )
    expand = jnp.einsum("lps,ls->p", basis_maps, node_sol, precision=highest)
    weighted = skel_feats * node_sol[:, None, :]
    pulled = jnp.einsum("lfs,lps->fp", weighted, basis_maps, precision=highest)
    grad_pts = solution[None, :] * (pulled - features * expand[None, :]) / skel_width
    toward = jnp.einsum("fp,lps->lfs", scaled, basis_maps, precision=highest)
    proj_sol = jnp.einsum("p,lps->ls", solution, basis_maps, precision=highest)
    grad_skel = node_sol[:, None, :] * (toward - skel_feats * proj_sol[:, None, :]) / skel_width
    skel_sum, _ = butterfly(list(grad_skel), None, levels, devices)
    routed = jnp.einsum("lfs,lsp->fp", jnp.stack(skel_sum), route, precision=highest)
    feat_grad = (grad_leaf + grad_pts + routed) / math.sqrt(points)

    low_grad = feat_grad.astype(jnp.bfloat16)
    grad_out = jnp.dot(low_grad, hid_two, preferred_element_type=jnp.float32)
    back_two = lax.dot_general(
        low_grad, w_out, (((0,), (0,)), ((), ())), preferred_element_type=jnp.float32
    )
    grad_two = (back_two * silu_slope(pre_two)).astype(jnp.bfloat16)
    grad_mid = lax.dot_general(
        hid_one, grad_two, (((0,), (0,)), ((), ())), preferred_element_type=jnp.float32
    )
    back_one = lax.dot_general(
        grad_two, w_mid, (((1,), (1,)), ((), ())), preferred_element_type=jnp.float32
    )
    grad_one = (back_one * silu_slope(pre_one)).astype(jnp.bfloat16)
    grad_in = lax.dot_general(
        inputs, grad_one, (((0,), (0,)), ((), ())), preferred_element_type=jnp.float32
    )
    stacked = lax.psum(jnp.concatenate([grad_in, grad_mid, grad_out], axis=0), "pts")
    n_in, n_mid = grad_in.shape[0], grad_mid.shape[0]
    grad_in = stacked[:n_in]
    grad_mid = stacked[n_in:n_in + n_mid]
    grad_out = stacked[n_in + n_mid:]
    return (solution, grad_in, grad_mid, grad_out)


def solution(mesh):
    in_specs = (P("pts", None), P("pts"), P(), P(), P(), P())
    out_specs = (P("pts"), P(), P(), P())
    return jax.shard_map(
        on_device, mesh=mesh, in_specs=in_specs, out_specs=out_specs, check_vma=False
    )
```

```python
import math

import jax
import jax.numpy as jnp
from jax import lax
from jax.sharding import PartitionSpec as P

ITERS = 2


noise_level = 1.0
highest = lax.Precision.HIGHEST


def kernel_block(left_feats, right_feats):
    cross_term = jnp.dot(
        left_feats.T, right_feats, precision=highest, preferred_element_type=jnp.float32
    )
    norm_left = jnp.sum(left_feats * left_feats, axis=0)
    norm_right = jnp.sum(right_feats * right_feats, axis=0)
    return jnp.exp(-0.5 * (norm_left[:, None] + norm_right[None, :] - 2.0 * cross_term))


def silu_slope(pre_act):
    sigmoid_val = jax.nn.sigmoid(pre_act)
    return sigmoid_val * (1.0 + pre_act * (1.0 - sigmoid_val))


def butterfly(parts, scalars, bits, devices, hook=None):
    parts = list(parts)
    for b in range(bits):
        live = [p.reshape(-1) for p in parts[b:]]
        if scalars is not None:
            live.append(scalars)
        payload = jnp.concatenate(live) if len(live) > 1 else live[0]
        recv = lax.ppermute(payload, "pts", [(i, i ^ (1 << b)) for i in range(devices)])
        total = payload + recv
        offset = 0
        for h in range(b, len(parts)):
            size = parts[h].size
            parts[h] = total[offset:offset + size].reshape(parts[h].shape)
            offset += size
        if scalars is not None:
            scalars = total[offset:]
        if hook is not None:
            scalars = hook(b, parts[b], scalars)
    return parts, scalars


def chain_orders(bits):
    if bits == 7:
        return [(0, 1, 3, 5, 2, 4, 6), (0, 3, 5, 1, 4, 6, 2), (0, 5, 1, 3, 6, 2, 4)]
    return [tuple(range(bits))]


def chained_all_reduce(flat, bits, devices, device_id):
    orders = chain_orders(bits)
    total = flat.shape[0]
    padded = -(-total // devices) * devices
    if padded != total:
        flat = jnp.concatenate([flat, jnp.zeros((padded - total,), flat.dtype)])
    units = padded // devices
    cuts = [units * c // len(orders) * devices for c in range(1, len(orders))]
    chunks = jnp.split(flat, cuts)
    for rnd in range(bits):
        for c, order in enumerate(orders):
            bit_index = order[rnd]
            half = chunks[c].shape[0] // 2
            upper = jnp.right_shift(device_id, bit_index) & 1
            keep = lax.dynamic_slice_in_dim(chunks[c], upper * half, half)
            send = lax.dynamic_slice_in_dim(chunks[c], (1 - upper) * half, half)
            chunks[c] = keep + xor_permute(send, bit_index, devices)
    for rnd in reversed(range(bits)):
        for c, order in enumerate(orders):
            bit_index = order[rnd]
            upper = jnp.right_shift(device_id, bit_index) & 1
            other = xor_permute(chunks[c], bit_index, devices)
            low = jnp.where(upper == 0, chunks[c], other)
            high = jnp.where(upper == 0, other, chunks[c])
            chunks[c] = jnp.concatenate([low, high])
    return jnp.concatenate(chunks)[:total]


def xor_permute(x, bit_index, devices):
    return lax.ppermute(x, "pts", [(i, i ^ (1 << bit_index)) for i in range(devices)])


def on_device(inputs, targets, skeletons, w_in, w_mid, w_out):
    devices = lax.axis_size("pts")
    levels = devices.bit_length() - 1
    device_id = lax.axis_index("pts")
    leaf_size = inputs.shape[0]
    skel_width = skeletons.shape[1]
    points = leaf_size * devices
    pre_one = jnp.dot(inputs, w_in, preferred_element_type=jnp.float32)
    hid_one = jax.nn.silu(pre_one).astype(jnp.bfloat16)
    pre_two = jnp.dot(hid_one, w_mid, preferred_element_type=jnp.float32)
    hid_two = jax.nn.silu(pre_two).astype(jnp.bfloat16)
    features = lax.dot_general(
        w_out, hid_two, (((1,), (1,)), ((), ())), preferred_element_type=jnp.float32
    )

    rows = jnp.stack(
        [
            lax.dynamic_index_in_dim(
                skeletons, jnp.right_shift(devices + device_id, height + 1) - 1, 0, False
            )
            for height in range(levels)
        ]
    )
    local_slots = rows - device_id * leaf_size
    route = (local_slots[:, :, None] == jnp.arange(leaf_size)[None, None, :]).astype(jnp.float32)
    pieces = jnp.einsum("fp,lsp->lfs", features, route, precision=highest)

    res_local = jnp.sum(targets * targets)
    skel_parts, scal = butterfly(list(pieces), res_local[None], levels, devices)
    res_norm = scal[0]
    skel_feats = jnp.stack(skel_parts)

    leaf_kernel = kernel_block(features, features)
    basis_maps = jnp.stack([kernel_block(features, skel_feats[h]) for h in range(levels)])

    def node_term(height, part, scalars):
        return scalars + jnp.concatenate(
            [jnp.zeros((1,), jnp.float32), (jnp.sum(part * part) / skel_width)[None]]
        )

    dir0 = targets
    near0 = jnp.dot(leaf_kernel, dir0, precision=highest, preferred_element_type=jnp.float32)
    proj0 = jnp.einsum("lps,p->ls", basis_maps, dir0, precision=highest)
    own0 = jnp.sum(dir0 * (noise_level * dir0 + near0))
    parts0, scal0 = butterfly(
        list(proj0), jnp.stack([own0, jnp.zeros((), jnp.float32)]), levels, devices, node_term
    )
    node0 = jnp.stack(parts0)
    curve0 = scal0[0] + scal0[1]
    step0 = res_norm / curve0
    far0 = jnp.einsum("lps,ls->p", basis_maps, node0, precision=highest) / skel_width
    image0 = noise_level * dir0 + near0 + far0
    sol_half = step0 * dir0
    resid = dir0 - step0 * image0

    near_res = jnp.dot(leaf_kernel, resid, precision=highest, preferred_element_type=jnp.float32)
    proj_res = jnp.einsum("lps,p->ls", basis_maps, resid, precision=highest)
    parts_r, scal_r = butterfly(list(proj_res), jnp.sum(resid * resid)[None], levels, devices)
    node_res = jnp.stack(parts_r)
    new_norm = scal_r[0]
    beta = new_norm / res_norm
    dir1 = resid + beta * dir0
    node1 = node_res + beta * node0
    near1 = near_res + beta * near0
    shares = jnp.sum(
        jnp.sum(node1 * node1, axis=1)
        / (skel_width * (2.0 ** jnp.arange(1, levels + 1, dtype=jnp.float32)))
    )
    own1 = jnp.sum(dir1 * (noise_level * dir1 + near1)) + shares
    _, scal1 = butterfly([], own1[None], levels, devices)
    curve1 = scal1[0]
    step1 = new_norm / curve1
    solution = sol_half + step1 * dir1
    node_sol = step0 * node0 + step1 * node1

    scaled = features * solution[None, :]
    kern_sol = jnp.dot(leaf_kernel, solution, precision=highest, preferred_element_type=jnp.float32)
    grad_leaf = solution[None, :] * (
        jnp.dot(scaled, leaf_kernel, precision=highest, preferred_element_type=jnp.float32)
        - features * kern_sol[None, :]
    )
    expand = jnp.einsum("lps,ls->p", basis_maps, node_sol, precision=highest)
    weighted = skel_feats * node_sol[:, None, :]
    pulled = jnp.einsum("lfs,lps->fp", weighted, basis_maps, precision=highest)
    grad_pts = solution[None, :] * (pulled - features * expand[None, :]) / skel_width
    toward = jnp.einsum("fp,lps->lfs", scaled, basis_maps, precision=highest)
    proj_sol = jnp.einsum("p,lps->ls", solution, basis_maps, precision=highest)
    grad_skel = node_sol[:, None, :] * (toward - skel_feats * proj_sol[:, None, :]) / skel_width
    skel_sum, _ = butterfly(list(grad_skel), None, levels, devices)
    routed = jnp.einsum("lfs,lsp->fp", jnp.stack(skel_sum), route, precision=highest)
    feat_grad = (grad_leaf + grad_pts + routed) / math.sqrt(points)

    low_grad = feat_grad.astype(jnp.bfloat16)
    grad_out = jnp.dot(low_grad, hid_two, preferred_element_type=jnp.float32)
    back_two = lax.dot_general(
        low_grad, w_out, (((0,), (0,)), ((), ())), preferred_element_type=jnp.float32
    )
    grad_two = (back_two * silu_slope(pre_two)).astype(jnp.bfloat16)
    grad_mid = lax.dot_general(
        hid_one, grad_two, (((0,), (0,)), ((), ())), preferred_element_type=jnp.float32
    )
    back_one = lax.dot_general(
        grad_two, w_mid, (((1,), (1,)), ((), ())), preferred_element_type=jnp.float32
    )
    grad_one = (back_one * silu_slope(pre_one)).astype(jnp.bfloat16)
    grad_in = lax.dot_general(
        inputs, grad_one, (((0,), (0,)), ((), ())), preferred_element_type=jnp.float32
    )
    grads = (grad_in, grad_mid, grad_out)
    flat = jnp.concatenate([g.reshape(-1) for g in grads])
    summed = chained_all_reduce(flat, levels, devices, device_id)
    outs = []
    offset = 0
    for g in grads:
        outs.append(summed[offset:offset + g.size].reshape(g.shape))
        offset += g.size
    grad_in, grad_mid, grad_out = outs
    return (solution, grad_in, grad_mid, grad_out)


def solution(mesh):
    in_specs = (P("pts", None), P("pts"), P(), P(), P(), P())
    out_specs = (P("pts"), P(), P(), P())
    return jax.shard_map(
        on_device, mesh=mesh, in_specs=in_specs, out_specs=out_specs, check_vma=False
    )
```

```python
import math

import jax
import jax.numpy as jnp
from jax import lax
from jax.sharding import PartitionSpec as P

ITERS = 2


noise_level = 1.0
highest = lax.Precision.HIGHEST


def kernel_block(left_feats, right_feats):
    cross_term = jnp.dot(
        left_feats.T, right_feats, precision=highest, preferred_element_type=jnp.float32
    )
    norm_left = jnp.sum(left_feats * left_feats, axis=0)
    norm_right = jnp.sum(right_feats * right_feats, axis=0)
    return jnp.exp(-0.5 * (norm_left[:, None] + norm_right[None, :] - 2.0 * cross_term))


def silu_slope(pre_act):
    sigmoid_val = jax.nn.sigmoid(pre_act)
    return sigmoid_val * (1.0 + pre_act * (1.0 - sigmoid_val))


def butterfly(parts, scalars, bits, devices, hook=None):
    parts = list(parts)
    for b in range(bits):
        live = [p.reshape(-1) for p in parts[b:]]
        if scalars is not None:
            live.append(scalars)
        payload = jnp.concatenate(live) if len(live) > 1 else live[0]
        recv = lax.ppermute(payload, "pts", [(i, i ^ (1 << b)) for i in range(devices)])
        total = payload + recv
        offset = 0
        for h in range(b, len(parts)):
            size = parts[h].size
            parts[h] = total[offset:offset + size].reshape(parts[h].shape)
            offset += size
        if scalars is not None:
            scalars = total[offset:]
        if hook is not None:
            scalars = hook(b, parts[b], scalars)
    return parts, scalars


def chain_orders(bits):
    if bits == 7:
        return [(0, 1, 3, 5, 2, 4, 6), (0, 3, 5, 1, 4, 6, 2), (0, 5, 1, 3, 6, 2, 4)]
    return [tuple(range(bits))]


def chained_all_reduce(flat, bits, devices, device_id):
    orders = chain_orders(bits)
    total = flat.shape[0]
    padded = -(-total // devices) * devices
    if padded != total:
        flat = jnp.concatenate([flat, jnp.zeros((padded - total,), flat.dtype)])
    units = padded // devices
    cuts = [units * c // len(orders) * devices for c in range(1, len(orders))]
    chunks = jnp.split(flat, cuts)
    for rnd in range(bits):
        for c, order in enumerate(orders):
            bit_index = order[rnd]
            half = chunks[c].shape[0] // 2
            upper = jnp.right_shift(device_id, bit_index) & 1
            keep = lax.dynamic_slice_in_dim(chunks[c], upper * half, half)
            send = lax.dynamic_slice_in_dim(chunks[c], (1 - upper) * half, half)
            chunks[c] = keep + xor_permute(send, bit_index, devices)
    for rnd in reversed(range(bits)):
        for c, order in enumerate(orders):
            bit_index = order[rnd]
            upper = jnp.right_shift(device_id, bit_index) & 1
            other = xor_permute(chunks[c], bit_index, devices)
            low = jnp.where(upper == 0, chunks[c], other)
            high = jnp.where(upper == 0, other, chunks[c])
            chunks[c] = jnp.concatenate([low, high])
    return jnp.concatenate(chunks)[:total]


def xor_permute(x, bit_index, devices):
    return lax.ppermute(x, "pts", [(i, i ^ (1 << bit_index)) for i in range(devices)])


def on_device(inputs, targets, skeletons, w_in, w_mid, w_out):
    devices = lax.axis_size("pts")
    levels = devices.bit_length() - 1
    device_id = lax.axis_index("pts")
    leaf_size = inputs.shape[0]
    skel_width = skeletons.shape[1]
    points = leaf_size * devices
    pre_one = jnp.dot(inputs, w_in, preferred_element_type=jnp.float32)
    hid_one = jax.nn.silu(pre_one).astype(jnp.bfloat16)
    pre_two = jnp.dot(hid_one, w_mid, preferred_element_type=jnp.float32)
    hid_two = jax.nn.silu(pre_two).astype(jnp.bfloat16)
    features = lax.dot_general(
        w_out, hid_two, (((1,), (1,)), ((), ())), preferred_element_type=jnp.float32
    )

    rows = jnp.stack(
        [
            lax.dynamic_index_in_dim(
                skeletons, jnp.right_shift(devices + device_id, height + 1) - 1, 0, False
            )
            for height in range(levels)
        ]
    )
    local_slots = rows - device_id * leaf_size
    route = (local_slots[:, :, None] == jnp.arange(leaf_size)[None, None, :]).astype(jnp.float32)
    pieces = jnp.einsum("fp,lsp->lfs", features, route, precision=highest)

    res_local = jnp.sum(targets * targets)
    skel_parts, scal = butterfly(list(pieces), res_local[None], levels, devices)
    res_norm = scal[0]
    skel_feats = jnp.stack(skel_parts)

    leaf_kernel, basis_maps = lax.optimization_barrier(
        (
            kernel_block(features, features),
            jnp.stack([kernel_block(features, skel_feats[h]) for h in range(levels)]),
        )
    )

    def node_term(height, part, scalars):
        return scalars + jnp.concatenate(
            [jnp.zeros((1,), jnp.float32), (jnp.sum(part * part) / skel_width)[None]]
        )

    dir0 = targets
    near0 = jnp.dot(leaf_kernel, dir0, precision=highest, preferred_element_type=jnp.float32)
    proj0 = jnp.einsum("lps,p->ls", basis_maps, dir0, precision=highest)
    own0 = jnp.sum(dir0 * (noise_level * dir0 + near0))
    parts0, scal0 = butterfly(
        list(proj0), jnp.stack([own0, jnp.zeros((), jnp.float32)]), levels, devices, node_term
    )
    node0 = jnp.stack(parts0)
    curve0 = scal0[0] + scal0[1]
    step0 = res_norm / curve0
    far0 = jnp.einsum("lps,ls->p", basis_maps, node0, precision=highest) / skel_width
    image0 = noise_level * dir0 + near0 + far0
    sol_half = step0 * dir0
    resid = dir0 - step0 * image0

    near_res = jnp.dot(leaf_kernel, resid, precision=highest, preferred_element_type=jnp.float32)
    proj_res = jnp.einsum("lps,p->ls", basis_maps, resid, precision=highest)
    parts_r, scal_r = butterfly(list(proj_res), jnp.sum(resid * resid)[None], levels, devices)
    node_res = jnp.stack(parts_r)
    new_norm = scal_r[0]
    beta = new_norm / res_norm
    dir1 = resid + beta * dir0
    node1 = node_res + beta * node0
    near1 = near_res + beta * near0
    shares = jnp.sum(
        jnp.sum(node1 * node1, axis=1)
        / (skel_width * (2.0 ** jnp.arange(1, levels + 1, dtype=jnp.float32)))
    )
    own1 = jnp.sum(dir1 * (noise_level * dir1 + near1)) + shares
    _, scal1 = butterfly([], own1[None], levels, devices)
    curve1 = scal1[0]
    step1 = new_norm / curve1
    solution = sol_half + step1 * dir1
    node_sol = step0 * node0 + step1 * node1

    scaled = features * solution[None, :]
    kern_sol = jnp.dot(leaf_kernel, solution, precision=highest, preferred_element_type=jnp.float32)
    grad_leaf = solution[None, :] * (
        jnp.dot(scaled, leaf_kernel, precision=highest, preferred_element_type=jnp.float32)
        - features * kern_sol[None, :]
    )
    expand = jnp.einsum("lps,ls->p", basis_maps, node_sol, precision=highest)
    weighted = skel_feats * node_sol[:, None, :]
    pulled = jnp.einsum("lfs,lps->fp", weighted, basis_maps, precision=highest)
    grad_pts = solution[None, :] * (pulled - features * expand[None, :]) / skel_width
    toward = jnp.einsum("fp,lps->lfs", scaled, basis_maps, precision=highest)
    proj_sol = jnp.einsum("p,lps->ls", solution, basis_maps, precision=highest)
    grad_skel = node_sol[:, None, :] * (toward - skel_feats * proj_sol[:, None, :]) / skel_width
    skel_sum, _ = butterfly(list(grad_skel), None, levels, devices)
    routed = jnp.einsum("lfs,lsp->fp", jnp.stack(skel_sum), route, precision=highest)
    feat_grad = (grad_leaf + grad_pts + routed) / math.sqrt(points)

    low_grad = feat_grad.astype(jnp.bfloat16)
    grad_out = jnp.dot(low_grad, hid_two, preferred_element_type=jnp.float32)
    back_two = lax.dot_general(
        low_grad, w_out, (((0,), (0,)), ((), ())), preferred_element_type=jnp.float32
    )
    grad_two = (back_two * silu_slope(pre_two)).astype(jnp.bfloat16)
    grad_mid = lax.dot_general(
        hid_one, grad_two, (((0,), (0,)), ((), ())), preferred_element_type=jnp.float32
    )
    back_one = lax.dot_general(
        grad_two, w_mid, (((1,), (1,)), ((), ())), preferred_element_type=jnp.float32
    )
    grad_one = (back_one * silu_slope(pre_one)).astype(jnp.bfloat16)
    grad_in = lax.dot_general(
        inputs, grad_one, (((0,), (0,)), ((), ())), preferred_element_type=jnp.float32
    )
    grads = (grad_in, grad_mid, grad_out)
    flat = jnp.concatenate([g.reshape(-1) for g in grads])
    summed = chained_all_reduce(flat, levels, devices, device_id)
    outs = []
    offset = 0
    for g in grads:
        outs.append(summed[offset:offset + g.size].reshape(g.shape))
        offset += g.size
    grad_in, grad_mid, grad_out = outs
    return (solution, grad_in, grad_mid, grad_out)


def solution(mesh):
    in_specs = (P("pts", None), P("pts"), P(), P(), P(), P())
    out_specs = (P("pts"), P(), P(), P())
    return jax.shard_map(
        on_device, mesh=mesh, in_specs=in_specs, out_specs=out_specs, check_vma=False
    )
```

```python
import math

import jax
import jax.numpy as jnp
from jax import lax
from jax.sharding import PartitionSpec as P

ITERS = 2


noise_level = 1.0
highest = lax.Precision.HIGHEST


def kernel_block(left_feats, right_feats):
    cross_term = jnp.dot(
        left_feats.T, right_feats, precision=highest, preferred_element_type=jnp.float32
    )
    norm_left = jnp.sum(left_feats * left_feats, axis=0)
    norm_right = jnp.sum(right_feats * right_feats, axis=0)
    return jnp.exp(-0.5 * (norm_left[:, None] + norm_right[None, :] - 2.0 * cross_term))


def silu_slope(pre_act):
    sigmoid_val = jax.nn.sigmoid(pre_act)
    return sigmoid_val * (1.0 + pre_act * (1.0 - sigmoid_val))


def butterfly(parts, scalars, bits, devices, hook=None):
    parts = list(parts)
    for b in range(bits):
        live = [p.reshape(-1) for p in parts[b:]]
        if scalars is not None:
            live.append(scalars)
        payload = jnp.concatenate(live) if len(live) > 1 else live[0]
        recv = lax.ppermute(payload, "pts", [(i, i ^ (1 << b)) for i in range(devices)])
        total = payload + recv
        offset = 0
        for h in range(b, len(parts)):
            size = parts[h].size
            parts[h] = total[offset:offset + size].reshape(parts[h].shape)
            offset += size
        if scalars is not None:
            scalars = total[offset:]
        if hook is not None:
            scalars = hook(b, parts[b], scalars)
    return parts, scalars


def chain_orders(bits):
    if bits == 7:
        return [(0, 1, 3, 5, 2, 4, 6), (0, 3, 5, 1, 4, 6, 2), (0, 5, 1, 3, 6, 2, 4)]
    return [tuple(range(bits))]


def chained_all_reduce(flat, bits, devices, device_id):
    orders = chain_orders(bits)
    total = flat.shape[0]
    padded = -(-total // devices) * devices
    if padded != total:
        flat = jnp.concatenate([flat, jnp.zeros((padded - total,), flat.dtype)])
    units = padded // devices
    cuts = [units * c // len(orders) * devices for c in range(1, len(orders))]
    chunks = jnp.split(flat, cuts)
    for rnd in range(bits):
        for c, order in enumerate(orders):
            bit_index = order[rnd]
            half = chunks[c].shape[0] // 2
            upper = jnp.right_shift(device_id, bit_index) & 1
            keep = lax.dynamic_slice_in_dim(chunks[c], upper * half, half)
            send = lax.dynamic_slice_in_dim(chunks[c], (1 - upper) * half, half)
            chunks[c] = keep + xor_permute(send, bit_index, devices)
    for rnd in reversed(range(bits)):
        for c, order in enumerate(orders):
            bit_index = order[rnd]
            upper = jnp.right_shift(device_id, bit_index) & 1
            other = xor_permute(chunks[c], bit_index, devices)
            low = jnp.where(upper == 0, chunks[c], other)
            high = jnp.where(upper == 0, other, chunks[c])
            chunks[c] = jnp.concatenate([low, high])
    return jnp.concatenate(chunks)[:total]


def xor_permute(x, bit_index, devices):
    return lax.ppermute(x, "pts", [(i, i ^ (1 << bit_index)) for i in range(devices)])


def on_device(inputs, targets, skeletons, w_in, w_mid, w_out):
    devices = lax.axis_size("pts")
    levels = devices.bit_length() - 1
    device_id = lax.axis_index("pts")
    leaf_size = inputs.shape[0]
    skel_width = skeletons.shape[1]
    points = leaf_size * devices
    pre_one = jnp.dot(inputs, w_in, preferred_element_type=jnp.float32)
    hid_one = jax.nn.silu(pre_one).astype(jnp.bfloat16)
    pre_two = jnp.dot(hid_one, w_mid, preferred_element_type=jnp.float32)
    hid_two = jax.nn.silu(pre_two).astype(jnp.bfloat16)
    features = lax.dot_general(
        w_out, hid_two, (((1,), (1,)), ((), ())), preferred_element_type=jnp.float32
    )

    rows = jnp.stack(
        [
            lax.dynamic_index_in_dim(
                skeletons, jnp.right_shift(devices + device_id, height + 1) - 1, 0, False
            )
            for height in range(levels)
        ]
    )
    local_slots = rows - device_id * leaf_size
    route = (local_slots[:, :, None] == jnp.arange(leaf_size)[None, None, :]).astype(jnp.float32)
    pieces = jnp.einsum("fp,lsp->lfs", features, route, precision=highest)

    res_local = jnp.sum(targets * targets)
    skel_parts, scal = butterfly(list(pieces), res_local[None], levels, devices)
    res_norm = scal[0]
    skel_feats = jnp.stack(skel_parts)

    leaf_kernel = kernel_block(features, features)
    basis_maps = jnp.stack([kernel_block(features, skel_feats[h]) for h in range(levels)])

    def node_term(height, part, scalars):
        return scalars + jnp.concatenate(
            [jnp.zeros((1,), jnp.float32), (jnp.sum(part * part) / skel_width)[None]]
        )

    dir0 = targets
    near0 = jnp.dot(leaf_kernel, dir0, precision=highest, preferred_element_type=jnp.float32)
    proj0 = jnp.einsum("lps,p->ls", basis_maps, dir0, precision=highest)
    own0 = jnp.sum(dir0 * (noise_level * dir0 + near0))
    parts0, scal0 = butterfly(
        list(proj0), jnp.stack([own0, jnp.zeros((), jnp.float32)]), levels, devices, node_term
    )
    node0 = jnp.stack(parts0)
    curve0 = scal0[0] + scal0[1]
    step0 = res_norm / curve0
    far0 = jnp.einsum("lps,ls->p", basis_maps, node0, precision=highest) / skel_width
    image0 = noise_level * dir0 + near0 + far0
    sol_half = step0 * dir0
    resid = dir0 - step0 * image0

    near_res = jnp.dot(leaf_kernel, resid, precision=highest, preferred_element_type=jnp.float32)
    proj_res = jnp.einsum("lps,p->ls", basis_maps, resid, precision=highest)
    own_res = jnp.stack(
        [
            jnp.sum(resid * resid),
            jnp.sum(resid * (noise_level * resid + near_res)),
            jnp.sum(resid * image0),
            jnp.zeros((), jnp.float32),
        ]
    )

    def node_term_res(height, part, scalars):
        return scalars + jnp.concatenate(
            [jnp.zeros((3,), jnp.float32), (jnp.sum(part * part) / skel_width)[None]]
        )

    parts_r, scal_r = butterfly(list(proj_res), own_res, levels, devices, node_term_res)
    node_res = jnp.stack(parts_r)
    new_norm = scal_r[0]
    beta = new_norm / res_norm
    dir1 = resid + beta * dir0
    node1 = node_res + beta * node0
    curve1 = (scal_r[1] + scal_r[3]) + 2.0 * beta * scal_r[2] + beta * beta * curve0
    step1 = new_norm / curve1
    solution = sol_half + step1 * dir1
    node_sol = step0 * node0 + step1 * node1

    scaled = features * solution[None, :]
    kern_sol = jnp.dot(leaf_kernel, solution, precision=highest, preferred_element_type=jnp.float32)
    grad_leaf = solution[None, :] * (
        jnp.dot(scaled, leaf_kernel, precision=highest, preferred_element_type=jnp.float32)
        - features * kern_sol[None, :]
    )
    expand = jnp.einsum("lps,ls->p", basis_maps, node_sol, precision=highest)
    weighted = skel_feats * node_sol[:, None, :]
    pulled = jnp.einsum("lfs,lps->fp", weighted, basis_maps, precision=highest)
    grad_pts = solution[None, :] * (pulled - features * expand[None, :]) / skel_width
    toward = jnp.einsum("fp,lps->lfs", scaled, basis_maps, precision=highest)
    proj_sol = jnp.einsum("p,lps->ls", solution, basis_maps, precision=highest)
    grad_skel = node_sol[:, None, :] * (toward - skel_feats * proj_sol[:, None, :]) / skel_width
    skel_sum, _ = butterfly(list(grad_skel), None, levels, devices)
    routed = jnp.einsum("lfs,lsp->fp", jnp.stack(skel_sum), route, precision=highest)
    feat_grad = (grad_leaf + grad_pts + routed) / math.sqrt(points)

    low_grad = feat_grad.astype(jnp.bfloat16)
    grad_out = jnp.dot(low_grad, hid_two, preferred_element_type=jnp.float32)
    back_two = lax.dot_general(
        low_grad, w_out, (((0,), (0,)), ((), ())), preferred_element_type=jnp.float32
    )
    grad_two = (back_two * silu_slope(pre_two)).astype(jnp.bfloat16)
    grad_mid = lax.dot_general(
        hid_one, grad_two, (((0,), (0,)), ((), ())), preferred_element_type=jnp.float32
    )
    back_one = lax.dot_general(
        grad_two, w_mid, (((1,), (1,)), ((), ())), preferred_element_type=jnp.float32
    )
    grad_one = (back_one * silu_slope(pre_one)).astype(jnp.bfloat16)
    grad_in = lax.dot_general(
        inputs, grad_one, (((0,), (0,)), ((), ())), preferred_element_type=jnp.float32
    )
    grads = (grad_in, grad_mid, grad_out)
    flat = jnp.concatenate([g.reshape(-1) for g in grads])
    summed = chained_all_reduce(flat, levels, devices, device_id)
    outs = []
    offset = 0
    for g in grads:
        outs.append(summed[offset:offset + g.size].reshape(g.shape))
        offset += g.size
    grad_in, grad_mid, grad_out = outs
    return (solution, grad_in, grad_mid, grad_out)


def solution(mesh):
    in_specs = (P("pts", None), P("pts"), P(), P(), P(), P())
    out_specs = (P("pts"), P(), P(), P())
    return jax.shard_map(
        on_device, mesh=mesh, in_specs=in_specs, out_specs=out_specs, check_vma=False
    )
```

```python
import math

import jax
import jax.numpy as jnp
from jax import lax
from jax.sharding import PartitionSpec as P

ITERS = 2


noise_level = 1.0
highest = lax.Precision.HIGHEST


def kernel_block(left_feats, right_feats):
    cross_term = jnp.dot(
        left_feats.T, right_feats, precision=highest, preferred_element_type=jnp.float32
    )
    norm_left = jnp.sum(left_feats * left_feats, axis=0)
    norm_right = jnp.sum(right_feats * right_feats, axis=0)
    return jnp.exp(-0.5 * (norm_left[:, None] + norm_right[None, :] - 2.0 * cross_term))


def silu_slope(pre_act):
    sigmoid_val = jax.nn.sigmoid(pre_act)
    return sigmoid_val * (1.0 + pre_act * (1.0 - sigmoid_val))


def butterfly(parts, scalars, bits, devices, hook=None):
    parts = list(parts)
    for b in range(bits):
        live = [p.reshape(-1) for p in parts[b:]]
        if scalars is not None:
            live.append(scalars)
        payload = jnp.concatenate(live) if len(live) > 1 else live[0]
        recv = lax.ppermute(payload, "pts", [(i, i ^ (1 << b)) for i in range(devices)])
        total = payload + recv
        offset = 0
        for h in range(b, len(parts)):
            size = parts[h].size
            parts[h] = total[offset:offset + size].reshape(parts[h].shape)
            offset += size
        if scalars is not None:
            scalars = total[offset:]
        if hook is not None:
            scalars = hook(b, parts[b], scalars)
    return parts, scalars


def chain_orders(bits):
    if bits == 7:
        return [(0, 1, 3, 5, 2, 4, 6), (0, 3, 5, 1, 4, 6, 2), (0, 5, 1, 3, 6, 2, 4)]
    return [tuple(range(bits))]


def chained_all_reduce(chunks, bits, devices, device_id):
    orders = chain_orders(bits)
    chunks = list(chunks)
    for rnd in range(bits):
        for c, order in enumerate(orders):
            bit_index = order[rnd]
            half = chunks[c].shape[1] // 2
            upper = jnp.right_shift(device_id, bit_index) & 1
            keep = lax.dynamic_slice_in_dim(chunks[c], upper * half, half, axis=1)
            send = lax.dynamic_slice_in_dim(chunks[c], (1 - upper) * half, half, axis=1)
            chunks[c] = keep + xor_permute(send, bit_index, devices)
    for rnd in reversed(range(bits)):
        for c, order in enumerate(orders):
            bit_index = order[rnd]
            upper = jnp.right_shift(device_id, bit_index) & 1
            other = xor_permute(chunks[c], bit_index, devices)
            low = jnp.where(upper == 0, chunks[c], other)
            high = jnp.where(upper == 0, other, chunks[c])
            chunks[c] = jnp.concatenate([low, high], axis=1)
    return chunks


def xor_permute(x, bit_index, devices):
    return lax.ppermute(x, "pts", [(i, i ^ (1 << bit_index)) for i in range(devices)])


def on_device(inputs, targets, skeletons, w_in, w_mid, w_out):
    devices = lax.axis_size("pts")
    levels = devices.bit_length() - 1
    device_id = lax.axis_index("pts")
    leaf_size = inputs.shape[0]
    skel_width = skeletons.shape[1]
    points = leaf_size * devices
    pre_one = jnp.dot(inputs, w_in, preferred_element_type=jnp.float32)
    hid_one = jax.nn.silu(pre_one).astype(jnp.bfloat16)
    pre_two = jnp.dot(hid_one, w_mid, preferred_element_type=jnp.float32)
    hid_two = jax.nn.silu(pre_two).astype(jnp.bfloat16)
    features = lax.dot_general(
        w_out, hid_two, (((1,), (1,)), ((), ())), preferred_element_type=jnp.float32
    )

    rows = jnp.stack(
        [
            lax.dynamic_index_in_dim(
                skeletons, jnp.right_shift(devices + device_id, height + 1) - 1, 0, False
            )
            for height in range(levels)
        ]
    )
    local_slots = rows - device_id * leaf_size
    route = (local_slots[:, :, None] == jnp.arange(leaf_size)[None, None, :]).astype(jnp.float32)
    pieces = jnp.einsum("fp,lsp->lfs", features, route, precision=highest)

    res_local = jnp.sum(targets * targets)
    skel_parts, scal = butterfly(list(pieces), res_local[None], levels, devices)
    res_norm = scal[0]
    skel_feats = jnp.stack(skel_parts)

    leaf_kernel = kernel_block(features, features)
    basis_maps = jnp.stack([kernel_block(features, skel_feats[h]) for h in range(levels)])

    def node_term(height, part, scalars):
        return scalars + jnp.concatenate(
            [jnp.zeros((1,), jnp.float32), (jnp.sum(part * part) / skel_width)[None]]
        )

    dir0 = targets
    near0 = jnp.dot(leaf_kernel, dir0, precision=highest, preferred_element_type=jnp.float32)
    proj0 = jnp.einsum("lps,p->ls", basis_maps, dir0, precision=highest)
    own0 = jnp.sum(dir0 * (noise_level * dir0 + near0))
    parts0, scal0 = butterfly(
        list(proj0), jnp.stack([own0, jnp.zeros((), jnp.float32)]), levels, devices, node_term
    )
    node0 = jnp.stack(parts0)
    curve0 = scal0[0] + scal0[1]
    step0 = res_norm / curve0
    far0 = jnp.einsum("lps,ls->p", basis_maps, node0, precision=highest) / skel_width
    image0 = noise_level * dir0 + near0 + far0
    sol_half = step0 * dir0
    resid = dir0 - step0 * image0

    near_res = jnp.dot(leaf_kernel, resid, precision=highest, preferred_element_type=jnp.float32)
    proj_res = jnp.einsum("lps,p->ls", basis_maps, resid, precision=highest)
    own_res = jnp.stack(
        [
            jnp.sum(resid * resid),
            jnp.sum(resid * (noise_level * resid + near_res)),
            jnp.sum(resid * image0),
            jnp.zeros((), jnp.float32),
        ]
    )

    def node_term_res(height, part, scalars):
        return scalars + jnp.concatenate(
            [jnp.zeros((3,), jnp.float32), (jnp.sum(part * part) / skel_width)[None]]
        )

    parts_r, scal_r = butterfly(list(proj_res), own_res, levels, devices, node_term_res)
    node_res = jnp.stack(parts_r)
    new_norm = scal_r[0]
    beta = new_norm / res_norm
    dir1 = resid + beta * dir0
    node1 = node_res + beta * node0
    curve1 = (scal_r[1] + scal_r[3]) + 2.0 * beta * scal_r[2] + beta * beta * curve0
    step1 = new_norm / curve1
    solution = sol_half + step1 * dir1
    node_sol = step0 * node0 + step1 * node1

    scaled = features * solution[None, :]
    kern_sol = jnp.dot(leaf_kernel, solution, precision=highest, preferred_element_type=jnp.float32)
    grad_leaf = solution[None, :] * (
        jnp.dot(scaled, leaf_kernel, precision=highest, preferred_element_type=jnp.float32)
        - features * kern_sol[None, :]
    )
    expand = jnp.einsum("lps,ls->p", basis_maps, node_sol, precision=highest)
    weighted = skel_feats * node_sol[:, None, :]
    pulled = jnp.einsum("lfs,lps->fp", weighted, basis_maps, precision=highest)
    grad_pts = solution[None, :] * (pulled - features * expand[None, :]) / skel_width
    toward = jnp.einsum("fp,lps->lfs", scaled, basis_maps, precision=highest)
    proj_sol = jnp.einsum("p,lps->ls", solution, basis_maps, precision=highest)
    grad_skel = node_sol[:, None, :] * (toward - skel_feats * proj_sol[:, None, :]) / skel_width
    skel_sum, _ = butterfly(list(grad_skel), None, levels, devices)
    routed = jnp.einsum("lfs,lsp->fp", jnp.stack(skel_sum), route, precision=highest)
    feat_grad = (grad_leaf + grad_pts + routed) / math.sqrt(points)

    low_grad = feat_grad.astype(jnp.bfloat16)
    grad_out = jnp.dot(low_grad, hid_two, preferred_element_type=jnp.float32)
    back_two = lax.dot_general(
        low_grad, w_out, (((0,), (0,)), ((), ())), preferred_element_type=jnp.float32
    )
    grad_two = (back_two * silu_slope(pre_two)).astype(jnp.bfloat16)
    grad_mid = lax.dot_general(
        hid_one, grad_two, (((0,), (0,)), ((), ())), preferred_element_type=jnp.float32
    )
    back_one = lax.dot_general(
        grad_two, w_mid, (((1,), (1,)), ((), ())), preferred_element_type=jnp.float32
    )
    grad_one = (back_one * silu_slope(pre_one)).astype(jnp.bfloat16)
    grad_in = lax.dot_general(
        inputs, grad_one, (((0,), (0,)), ((), ())), preferred_element_type=jnp.float32
    )
    rows = grad_in.shape[0] + grad_mid.shape[0] + grad_out.shape[0]
    n_chains = len(chain_orders(levels))
    cut = [(rows * c // n_chains) // 8 * 8 for c in range(n_chains + 1)]
    cut[-1] = rows
    stacked = jnp.concatenate([grad_mid, grad_in, grad_out], axis=0)
    pieces = chained_all_reduce(
        [stacked[cut[c]:cut[c + 1]] for c in range(n_chains)], levels, devices, device_id
    )
    stacked = jnp.concatenate(pieces, axis=0)
    n_mid, n_in = grad_mid.shape[0], grad_in.shape[0]
    grad_mid = stacked[:n_mid]
    grad_in = stacked[n_mid:n_mid + n_in]
    grad_out = stacked[n_mid + n_in:]
    return (solution, grad_in, grad_mid, grad_out)


def solution(mesh):
    in_specs = (P("pts", None), P("pts"), P(), P(), P(), P())
    out_specs = (P("pts"), P(), P(), P())
    return jax.shard_map(
        on_device, mesh=mesh, in_specs=in_specs, out_specs=out_specs, check_vma=False
    )
```

```python
import math

import jax
import jax.numpy as jnp
from jax import lax
from jax.sharding import PartitionSpec as P

ITERS = 2


noise_level = 1.0
highest = lax.Precision.HIGHEST


def kernel_block(left_feats, right_feats):
    cross_term = jnp.dot(
        left_feats.T, right_feats, precision=highest, preferred_element_type=jnp.float32
    )
    norm_left = jnp.sum(left_feats * left_feats, axis=0)
    norm_right = jnp.sum(right_feats * right_feats, axis=0)
    return jnp.exp(-0.5 * (norm_left[:, None] + norm_right[None, :] - 2.0 * cross_term))


def silu_slope(pre_act):
    sigmoid_val = jax.nn.sigmoid(pre_act)
    return sigmoid_val * (1.0 + pre_act * (1.0 - sigmoid_val))


def kernel_times(kernel, vec):
    return jnp.sum(kernel * vec[None, :], axis=1)


def project(basis, vec):
    return jnp.sum(basis * vec[None, :, None], axis=1)


def spread(basis, node_vals):
    return jnp.sum(basis * node_vals[:, None, :], axis=(0, 2))


def butterfly(parts, scalars, bits, devices, hook=None):
    parts = list(parts)
    for b in range(bits):
        live = [p.reshape(-1) for p in parts[b:]]
        if scalars is not None:
            live.append(scalars)
        payload = jnp.concatenate(live) if len(live) > 1 else live[0]
        recv = lax.ppermute(payload, "pts", [(i, i ^ (1 << b)) for i in range(devices)])
        total = payload + recv
        offset = 0
        for h in range(b, len(parts)):
            size = parts[h].size
            parts[h] = total[offset:offset + size].reshape(parts[h].shape)
            offset += size
        if scalars is not None:
            scalars = total[offset:]
        if hook is not None:
            scalars = hook(b, parts[b], scalars)
    return parts, scalars


def chain_orders(bits):
    if bits == 7:
        return [(0, 1, 3, 5, 2, 4, 6), (0, 3, 5, 1, 4, 6, 2), (0, 5, 1, 3, 6, 2, 4)]
    return [tuple(range(bits))]


def chained_all_reduce(chunks, bits, devices, device_id):
    orders = chain_orders(bits)
    chunks = list(chunks)
    for rnd in range(bits):
        for c, order in enumerate(orders):
            bit_index = order[rnd]
            half = chunks[c].shape[1] // 2
            upper = jnp.right_shift(device_id, bit_index) & 1
            keep = lax.dynamic_slice_in_dim(chunks[c], upper * half, half, axis=1)
            send = lax.dynamic_slice_in_dim(chunks[c], (1 - upper) * half, half, axis=1)
            chunks[c] = keep + xor_permute(send, bit_index, devices)
    for rnd in reversed(range(bits)):
        for c, order in enumerate(orders):
            bit_index = order[rnd]
            upper = jnp.right_shift(device_id, bit_index) & 1
            other = xor_permute(chunks[c], bit_index, devices)
            low = jnp.where(upper == 0, chunks[c], other)
            high = jnp.where(upper == 0, other, chunks[c])
            chunks[c] = jnp.concatenate([low, high], axis=1)
    return chunks


def xor_permute(x, bit_index, devices):
    return lax.ppermute(x, "pts", [(i, i ^ (1 << bit_index)) for i in range(devices)])


def on_device(inputs, targets, skeletons, w_in, w_mid, w_out):
    devices = lax.axis_size("pts")
    levels = devices.bit_length() - 1
    device_id = lax.axis_index("pts")
    leaf_size = inputs.shape[0]
    skel_width = skeletons.shape[1]
    points = leaf_size * devices
    pre_one = jnp.dot(inputs, w_in, preferred_element_type=jnp.float32)
    hid_one = jax.nn.silu(pre_one).astype(jnp.bfloat16)
    pre_two = jnp.dot(hid_one, w_mid, preferred_element_type=jnp.float32)
    hid_two = jax.nn.silu(pre_two).astype(jnp.bfloat16)
    features = lax.dot_general(
        w_out, hid_two, (((1,), (1,)), ((), ())), preferred_element_type=jnp.float32
    )

    rows = jnp.stack(
        [
            lax.dynamic_index_in_dim(
                skeletons, jnp.right_shift(devices + device_id, height + 1) - 1, 0, False
            )
            for height in range(levels)
        ]
    )
    local_slots = rows - device_id * leaf_size
    route = (local_slots[:, :, None] == jnp.arange(leaf_size)[None, None, :]).astype(jnp.float32)
    pieces = jnp.einsum("fp,lsp->lfs", features, route, precision=highest)

    res_local = jnp.sum(targets * targets)
    skel_parts, scal = butterfly(list(pieces), res_local[None], levels, devices)
    res_norm = scal[0]
    skel_feats = jnp.stack(skel_parts)

    leaf_kernel = kernel_block(features, features)
    basis_maps = jnp.stack([kernel_block(features, skel_feats[h]) for h in range(levels)])

    def node_term(height, part, scalars):
        return scalars + jnp.concatenate(
            [jnp.zeros((1,), jnp.float32), (jnp.sum(part * part) / skel_width)[None]]
        )

    dir0 = targets
    near0 = kernel_times(leaf_kernel, dir0)
    proj0 = project(basis_maps, dir0)
    own0 = jnp.sum(dir0 * (noise_level * dir0 + near0))
    parts0, scal0 = butterfly(
        list(proj0), jnp.stack([own0, jnp.zeros((), jnp.float32)]), levels, devices, node_term
    )
    node0 = jnp.stack(parts0)
    curve0 = scal0[0] + scal0[1]
    step0 = res_norm / curve0
    far0 = spread(basis_maps, node0) / skel_width
    image0 = noise_level * dir0 + near0 + far0
    sol_half = step0 * dir0
    resid = dir0 - step0 * image0

    near_res = kernel_times(leaf_kernel, resid)
    proj_res = project(basis_maps, resid)
    own_res = jnp.stack(
        [
            jnp.sum(resid * resid),
            jnp.sum(resid * (noise_level * resid + near_res)),
            jnp.sum(resid * image0),
            jnp.zeros((), jnp.float32),
        ]
    )

    def node_term_res(height, part, scalars):
        return scalars + jnp.concatenate(
            [jnp.zeros((3,), jnp.float32), (jnp.sum(part * part) / skel_width)[None]]
        )

    parts_r, scal_r = butterfly(list(proj_res), own_res, levels, devices, node_term_res)
    node_res = jnp.stack(parts_r)
    new_norm = scal_r[0]
    beta = new_norm / res_norm
    dir1 = resid + beta * dir0
    node1 = node_res + beta * node0
    curve1 = (scal_r[1] + scal_r[3]) + 2.0 * beta * scal_r[2] + beta * beta * curve0
    step1 = new_norm / curve1
    solution = sol_half + step1 * dir1
    node_sol = step0 * node0 + step1 * node1

    scaled = features * solution[None, :]
    kern_sol = kernel_times(leaf_kernel, solution)
    grad_leaf = solution[None, :] * (
        jnp.dot(scaled, leaf_kernel, precision=highest, preferred_element_type=jnp.float32)
        - features * kern_sol[None, :]
    )
    expand = spread(basis_maps, node_sol)
    weighted = skel_feats * node_sol[:, None, :]
    pulled = jnp.einsum("lfs,lps->fp", weighted, basis_maps, precision=highest)
    grad_pts = solution[None, :] * (pulled - features * expand[None, :]) / skel_width
    toward = jnp.einsum("fp,lps->lfs", scaled, basis_maps, precision=highest)
    proj_sol = project(basis_maps, solution)
    grad_skel = node_sol[:, None, :] * (toward - skel_feats * proj_sol[:, None, :]) / skel_width
    skel_sum, _ = butterfly(list(grad_skel), None, levels, devices)
    routed = jnp.einsum("lfs,lsp->fp", jnp.stack(skel_sum), route, precision=highest)
    feat_grad = (grad_leaf + grad_pts + routed) / math.sqrt(points)

    low_grad = feat_grad.astype(jnp.bfloat16)
    grad_out = jnp.dot(low_grad, hid_two, preferred_element_type=jnp.float32)
    back_two = lax.dot_general(
        low_grad, w_out, (((0,), (0,)), ((), ())), preferred_element_type=jnp.float32
    )
    grad_two = (back_two * silu_slope(pre_two)).astype(jnp.bfloat16)
    grad_mid = lax.dot_general(
        hid_one, grad_two, (((0,), (0,)), ((), ())), preferred_element_type=jnp.float32
    )
    back_one = lax.dot_general(
        grad_two, w_mid, (((1,), (1,)), ((), ())), preferred_element_type=jnp.float32
    )
    grad_one = (back_one * silu_slope(pre_one)).astype(jnp.bfloat16)
    grad_in = lax.dot_general(
        inputs, grad_one, (((0,), (0,)), ((), ())), preferred_element_type=jnp.float32
    )
    rows = grad_in.shape[0] + grad_mid.shape[0] + grad_out.shape[0]
    n_chains = len(chain_orders(levels))
    cut = [(rows * c // n_chains) // 8 * 8 for c in range(n_chains + 1)]
    cut[-1] = rows
    stacked = jnp.concatenate([grad_mid, grad_in, grad_out], axis=0)
    pieces = chained_all_reduce(
        [stacked[cut[c]:cut[c + 1]] for c in range(n_chains)], levels, devices, device_id
    )
    stacked = jnp.concatenate(pieces, axis=0)
    n_mid, n_in = grad_mid.shape[0], grad_in.shape[0]
    grad_mid = stacked[:n_mid]
    grad_in = stacked[n_mid:n_mid + n_in]
    grad_out = stacked[n_mid + n_in:]
    return (solution, grad_in, grad_mid, grad_out)


def solution(mesh):
    in_specs = (P("pts", None), P("pts"), P(), P(), P(), P())
    out_specs = (P("pts"), P(), P(), P())
    return jax.shard_map(
        on_device, mesh=mesh, in_specs=in_specs, out_specs=out_specs, check_vma=False
    )
```

```python
import math

import jax
import jax.numpy as jnp
from jax import lax
from jax.sharding import PartitionSpec as P

ITERS = 2


noise_level = 1.0
highest = lax.Precision.HIGHEST


def kernel_block(left_feats, right_feats):
    cross_term = jnp.dot(
        left_feats.T, right_feats, precision=highest, preferred_element_type=jnp.float32
    )
    norm_left = jnp.sum(left_feats * left_feats, axis=0)
    norm_right = jnp.sum(right_feats * right_feats, axis=0)
    return jnp.exp(-0.5 * (norm_left[:, None] + norm_right[None, :] - 2.0 * cross_term))


def silu_slope(pre_act):
    sigmoid_val = jax.nn.sigmoid(pre_act)
    return sigmoid_val * (1.0 + pre_act * (1.0 - sigmoid_val))


def kernel_times(kernel, vec):
    return jnp.sum(kernel * vec[None, :], axis=1)


def project(basis, vec):
    return jnp.sum(basis * vec[None, :, None], axis=1)


def spread(basis, node_vals):
    return jnp.sum(basis * node_vals[:, None, :], axis=(0, 2))


def butterfly(parts, scalars, bits, devices, hook=None):
    parts = list(parts)
    width = parts[0].shape[1] if parts else scalars.shape[0]
    count = None if scalars is None else scalars.shape[0]
    for b in range(bits):
        live = list(parts[b:])
        if scalars is not None:
            live.append(jnp.pad(scalars, (0, width - count))[None, :])
        payload = jnp.concatenate(live, axis=0) if len(live) > 1 else live[0]
        recv = lax.ppermute(payload, "pts", [(i, i ^ (1 << b)) for i in range(devices)])
        total = payload + recv
        offset = 0
        for h in range(b, len(parts)):
            size = parts[h].shape[0]
            parts[h] = total[offset:offset + size]
            offset += size
        if scalars is not None:
            scalars = total[offset, :count]
        if hook is not None:
            scalars = hook(b, parts[b], scalars)
    return parts, scalars


def chain_orders(bits):
    if bits == 7:
        return [(0, 1, 3, 5, 2, 4, 6), (0, 3, 5, 1, 4, 6, 2), (0, 5, 1, 3, 6, 2, 4)]
    return [tuple(range(bits))]


def chained_all_reduce(chunks, bits, devices, device_id):
    orders = chain_orders(bits)
    chunks = list(chunks)
    for rnd in range(bits):
        for c, order in enumerate(orders):
            bit_index = order[rnd]
            half = chunks[c].shape[1] // 2
            upper = jnp.right_shift(device_id, bit_index) & 1
            keep = lax.dynamic_slice_in_dim(chunks[c], upper * half, half, axis=1)
            send = lax.dynamic_slice_in_dim(chunks[c], (1 - upper) * half, half, axis=1)
            chunks[c] = keep + xor_permute(send, bit_index, devices)
    for rnd in reversed(range(bits)):
        for c, order in enumerate(orders):
            bit_index = order[rnd]
            upper = jnp.right_shift(device_id, bit_index) & 1
            other = xor_permute(chunks[c], bit_index, devices)
            low = jnp.where(upper == 0, chunks[c], other)
            high = jnp.where(upper == 0, other, chunks[c])
            chunks[c] = jnp.concatenate([low, high], axis=1)
    return chunks


def xor_permute(x, bit_index, devices):
    return lax.ppermute(x, "pts", [(i, i ^ (1 << bit_index)) for i in range(devices)])


def on_device(inputs, targets, skeletons, w_in, w_mid, w_out):
    devices = lax.axis_size("pts")
    levels = devices.bit_length() - 1
    device_id = lax.axis_index("pts")
    leaf_size = inputs.shape[0]
    skel_width = skeletons.shape[1]
    points = leaf_size * devices
    pre_one = jnp.dot(inputs, w_in, preferred_element_type=jnp.float32)
    hid_one = jax.nn.silu(pre_one).astype(jnp.bfloat16)
    pre_two = jnp.dot(hid_one, w_mid, preferred_element_type=jnp.float32)
    hid_two = jax.nn.silu(pre_two).astype(jnp.bfloat16)
    features = lax.dot_general(
        w_out, hid_two, (((1,), (1,)), ((), ())), preferred_element_type=jnp.float32
    )

    rows = jnp.stack(
        [
            lax.dynamic_index_in_dim(
                skeletons, jnp.right_shift(devices + device_id, height + 1) - 1, 0, False
            )
            for height in range(levels)
        ]
    )
    local_slots = rows - device_id * leaf_size
    route = (local_slots[:, :, None] == jnp.arange(leaf_size)[None, None, :]).astype(jnp.float32)
    pieces = jnp.einsum("fp,lsp->lfs", features, route, precision=highest)

    res_local = jnp.sum(targets * targets)
    skel_parts, scal = butterfly(list(pieces), res_local[None], levels, devices)
    res_norm = scal[0]
    skel_feats = jnp.stack(skel_parts)

    leaf_kernel = kernel_block(features, features)
    basis_maps = jnp.stack([kernel_block(features, skel_feats[h]) for h in range(levels)])

    def node_term(height, part, scalars):
        return scalars + jnp.concatenate(
            [jnp.zeros((1,), jnp.float32), (jnp.sum(part * part) / skel_width)[None]]
        )

    dir0 = targets
    near0 = kernel_times(leaf_kernel, dir0)
    proj0 = project(basis_maps, dir0)
    own0 = jnp.sum(dir0 * (noise_level * dir0 + near0))
    parts0, scal0 = butterfly(
        list(proj0[:, None, :]), jnp.stack([own0, jnp.zeros((), jnp.float32)]), levels, devices,
        node_term,
    )
    node0 = jnp.concatenate(parts0, axis=0)
    curve0 = scal0[0] + scal0[1]
    step0 = res_norm / curve0
    far0 = spread(basis_maps, node0) / skel_width
    image0 = noise_level * dir0 + near0 + far0
    sol_half = step0 * dir0
    resid = dir0 - step0 * image0

    near_res = kernel_times(leaf_kernel, resid)
    proj_res = project(basis_maps, resid)
    own_res = jnp.stack(
        [
            jnp.sum(resid * resid),
            jnp.sum(resid * (noise_level * resid + near_res)),
            jnp.sum(resid * image0),
            jnp.zeros((), jnp.float32),
        ]
    )

    def node_term_res(height, part, scalars):
        return scalars + jnp.concatenate(
            [jnp.zeros((3,), jnp.float32), (jnp.sum(part * part) / skel_width)[None]]
        )

    parts_r, scal_r = butterfly(
        list(proj_res[:, None, :]), own_res, levels, devices, node_term_res
    )
    node_res = jnp.concatenate(parts_r, axis=0)
    new_norm = scal_r[0]
    beta = new_norm / res_norm
    dir1 = resid + beta * dir0
    node1 = node_res + beta * node0
    curve1 = (scal_r[1] + scal_r[3]) + 2.0 * beta * scal_r[2] + beta * beta * curve0
    step1 = new_norm / curve1
    solution = sol_half + step1 * dir1
    node_sol = step0 * node0 + step1 * node1

    scaled = features * solution[None, :]
    kern_sol = kernel_times(leaf_kernel, solution)
    grad_leaf = solution[None, :] * (
        jnp.dot(scaled, leaf_kernel, precision=highest, preferred_element_type=jnp.float32)
        - features * kern_sol[None, :]
    )
    expand = spread(basis_maps, node_sol)
    weighted = skel_feats * node_sol[:, None, :]
    pulled = jnp.einsum("lfs,lps->fp", weighted, basis_maps, precision=highest)
    grad_pts = solution[None, :] * (pulled - features * expand[None, :]) / skel_width
    toward = jnp.einsum("fp,lps->lfs", scaled, basis_maps, precision=highest)
    proj_sol = project(basis_maps, solution)
    grad_skel = node_sol[:, None, :] * (toward - skel_feats * proj_sol[:, None, :]) / skel_width
    skel_sum, _ = butterfly(list(grad_skel), None, levels, devices)
    routed = jnp.einsum("lfs,lsp->fp", jnp.stack(skel_sum), route, precision=highest)
    feat_grad = (grad_leaf + grad_pts + routed) / math.sqrt(points)

    low_grad = feat_grad.astype(jnp.bfloat16)
    grad_out = jnp.dot(low_grad, hid_two, preferred_element_type=jnp.float32)
    back_two = lax.dot_general(
        low_grad, w_out, (((0,), (0,)), ((), ())), preferred_element_type=jnp.float32
    )
    grad_two = (back_two * silu_slope(pre_two)).astype(jnp.bfloat16)
    grad_mid = lax.dot_general(
        hid_one, grad_two, (((0,), (0,)), ((), ())), preferred_element_type=jnp.float32
    )
    back_one = lax.dot_general(
        grad_two, w_mid, (((1,), (1,)), ((), ())), preferred_element_type=jnp.float32
    )
    grad_one = (back_one * silu_slope(pre_one)).astype(jnp.bfloat16)
    grad_in = lax.dot_general(
        inputs, grad_one, (((0,), (0,)), ((), ())), preferred_element_type=jnp.float32
    )
    rows = grad_in.shape[0] + grad_mid.shape[0] + grad_out.shape[0]
    n_chains = len(chain_orders(levels))
    cut = [(rows * c // n_chains) // 8 * 8 for c in range(n_chains + 1)]
    cut[-1] = rows
    stacked = jnp.concatenate([grad_mid, grad_in, grad_out], axis=0)
    pieces = chained_all_reduce(
        [stacked[cut[c]:cut[c + 1]] for c in range(n_chains)], levels, devices, device_id
    )
    stacked = jnp.concatenate(pieces, axis=0)
    n_mid, n_in = grad_mid.shape[0], grad_in.shape[0]
    grad_mid = stacked[:n_mid]
    grad_in = stacked[n_mid:n_mid + n_in]
    grad_out = stacked[n_mid + n_in:]
    return (solution, grad_in, grad_mid, grad_out)


def solution(mesh):
    in_specs = (P("pts", None), P("pts"), P(), P(), P(), P())
    out_specs = (P("pts"), P(), P(), P())
    return jax.shard_map(
        on_device, mesh=mesh, in_specs=in_specs, out_specs=out_specs, check_vma=False
    )
```

```python
import math

import jax
import jax.numpy as jnp
from jax import lax
from jax.sharding import PartitionSpec as P

ITERS = 2


noise_level = 1.0
highest = lax.Precision.HIGHEST
high = lax.Precision.HIGH


def kernel_block(left_feats, right_feats):
    cross_term = jnp.dot(
        left_feats.T, right_feats, precision=highest, preferred_element_type=jnp.float32
    )
    norm_left = jnp.sum(left_feats * left_feats, axis=0)
    norm_right = jnp.sum(right_feats * right_feats, axis=0)
    return jnp.exp(-0.5 * (norm_left[:, None] + norm_right[None, :] - 2.0 * cross_term))


def silu_slope(pre_act):
    sigmoid_val = jax.nn.sigmoid(pre_act)
    return sigmoid_val * (1.0 + pre_act * (1.0 - sigmoid_val))


def kernel_times(kernel, vec):
    return jnp.sum(kernel * vec[None, :], axis=1)


def project(basis, vec):
    return jnp.sum(basis * vec[None, :, None], axis=1)


def spread(basis, node_vals):
    return jnp.sum(basis * node_vals[:, None, :], axis=(0, 2))


def butterfly(parts, scalars, bits, devices, hook=None):
    parts = list(parts)
    for b in range(bits):
        live = [p.reshape(-1) for p in parts[b:]]
        if scalars is not None:
            live.append(scalars)
        payload = jnp.concatenate(live) if len(live) > 1 else live[0]
        recv = lax.ppermute(payload, "pts", [(i, i ^ (1 << b)) for i in range(devices)])
        total = payload + recv
        offset = 0
        for h in range(b, len(parts)):
            size = parts[h].size
            parts[h] = total[offset:offset + size].reshape(parts[h].shape)
            offset += size
        if scalars is not None:
            scalars = total[offset:]
        if hook is not None:
            scalars = hook(b, parts[b], scalars)
    return parts, scalars


def chain_orders(bits):
    if bits == 7:
        return [(0, 1, 3, 5, 2, 4, 6), (0, 3, 5, 1, 4, 6, 2), (0, 5, 1, 3, 6, 2, 4)]
    return [tuple(range(bits))]


def chained_all_reduce(chunks, bits, devices, device_id):
    orders = chain_orders(bits)
    chunks = list(chunks)
    for rnd in range(bits):
        for c, order in enumerate(orders):
            bit_index = order[rnd]
            half = chunks[c].shape[1] // 2
            upper = jnp.right_shift(device_id, bit_index) & 1
            keep = lax.dynamic_slice_in_dim(chunks[c], upper * half, half, axis=1)
            send = lax.dynamic_slice_in_dim(chunks[c], (1 - upper) * half, half, axis=1)
            chunks[c] = keep + xor_permute(send, bit_index, devices)
    for rnd in reversed(range(bits)):
        for c, order in enumerate(orders):
            bit_index = order[rnd]
            upper = jnp.right_shift(device_id, bit_index) & 1
            other = xor_permute(chunks[c], bit_index, devices)
            low = jnp.where(upper == 0, chunks[c], other)
            high = jnp.where(upper == 0, other, chunks[c])
            chunks[c] = jnp.concatenate([low, high], axis=1)
    return chunks


def xor_permute(x, bit_index, devices):
    return lax.ppermute(x, "pts", [(i, i ^ (1 << bit_index)) for i in range(devices)])


def on_device(inputs, targets, skeletons, w_in, w_mid, w_out):
    devices = lax.axis_size("pts")
    levels = devices.bit_length() - 1
    device_id = lax.axis_index("pts")
    leaf_size = inputs.shape[0]
    skel_width = skeletons.shape[1]
    points = leaf_size * devices
    pre_one = jnp.dot(inputs, w_in, preferred_element_type=jnp.float32)
    hid_one = jax.nn.silu(pre_one).astype(jnp.bfloat16)
    pre_two = jnp.dot(hid_one, w_mid, preferred_element_type=jnp.float32)
    hid_two = jax.nn.silu(pre_two).astype(jnp.bfloat16)
    features = lax.dot_general(
        w_out, hid_two, (((1,), (1,)), ((), ())), preferred_element_type=jnp.float32
    )

    rows = jnp.stack(
        [
            lax.dynamic_index_in_dim(
                skeletons, jnp.right_shift(devices + device_id, height + 1) - 1, 0, False
            )
            for height in range(levels)
        ]
    )
    local_slots = rows - device_id * leaf_size
    route = (local_slots[:, :, None] == jnp.arange(leaf_size)[None, None, :]).astype(jnp.float32)
    pieces = jnp.einsum("fp,lsp->lfs", features, route, precision=highest)

    res_local = jnp.sum(targets * targets)
    skel_parts, scal = butterfly(list(pieces), res_local[None], levels, devices)
    res_norm = scal[0]
    skel_feats = jnp.stack(skel_parts)

    leaf_kernel = kernel_block(features, features)
    basis_maps = jnp.stack([kernel_block(features, skel_feats[h]) for h in range(levels)])

    def node_term(height, part, scalars):
        return scalars + jnp.concatenate(
            [jnp.zeros((1,), jnp.float32), (jnp.sum(part * part) / skel_width)[None]]
        )

    dir0 = targets
    near0 = kernel_times(leaf_kernel, dir0)
    proj0 = project(basis_maps, dir0)
    own0 = jnp.sum(dir0 * (noise_level * dir0 + near0))
    parts0, scal0 = butterfly(
        list(proj0), jnp.stack([own0, jnp.zeros((), jnp.float32)]), levels, devices, node_term
    )
    node0 = jnp.stack(parts0)
    curve0 = scal0[0] + scal0[1]
    step0 = res_norm / curve0
    far0 = spread(basis_maps, node0) / skel_width
    image0 = noise_level * dir0 + near0 + far0
    sol_half = step0 * dir0
    resid = dir0 - step0 * image0

    near_res = kernel_times(leaf_kernel, resid)
    proj_res = project(basis_maps, resid)
    own_res = jnp.stack(
        [
            jnp.sum(resid * resid),
            jnp.sum(resid * (noise_level * resid + near_res)),
            jnp.sum(resid * image0),
            jnp.zeros((), jnp.float32),
        ]
    )

    def node_term_res(height, part, scalars):
        return scalars + jnp.concatenate(
            [jnp.zeros((3,), jnp.float32), (jnp.sum(part * part) / skel_width)[None]]
        )

    parts_r, scal_r = butterfly(list(proj_res), own_res, levels, devices, node_term_res)
    node_res = jnp.stack(parts_r)
    new_norm = scal_r[0]
    beta = new_norm / res_norm
    dir1 = resid + beta * dir0
    node1 = node_res + beta * node0
    curve1 = (scal_r[1] + scal_r[3]) + 2.0 * beta * scal_r[2] + beta * beta * curve0
    step1 = new_norm / curve1
    solution = sol_half + step1 * dir1
    node_sol = step0 * node0 + step1 * node1

    scaled = features * solution[None, :]
    kern_sol = kernel_times(leaf_kernel, solution)
    grad_leaf = solution[None, :] * (
        jnp.dot(scaled, leaf_kernel, precision=high, preferred_element_type=jnp.float32)
        - features * kern_sol[None, :]
    )
    expand = spread(basis_maps, node_sol)
    weighted = skel_feats * node_sol[:, None, :]
    pulled = jnp.einsum("lfs,lps->fp", weighted, basis_maps, precision=high)
    grad_pts = solution[None, :] * (pulled - features * expand[None, :]) / skel_width
    toward = jnp.einsum("fp,lps->lfs", scaled, basis_maps, precision=high)
    proj_sol = project(basis_maps, solution)
    grad_skel = node_sol[:, None, :] * (toward - skel_feats * proj_sol[:, None, :]) / skel_width
    skel_sum, _ = butterfly(list(grad_skel), None, levels, devices)
    routed = jnp.einsum("lfs,lsp->fp", jnp.stack(skel_sum), route, precision=high)
    feat_grad = (grad_leaf + grad_pts + routed) / math.sqrt(points)

    low_grad = feat_grad.astype(jnp.bfloat16)
    grad_out = jnp.dot(low_grad, hid_two, preferred_element_type=jnp.float32)
    back_two = lax.dot_general(
        low_grad, w_out, (((0,), (0,)), ((), ())), preferred_element_type=jnp.float32
    )
    grad_two = (back_two * silu_slope(pre_two)).astype(jnp.bfloat16)
    grad_mid = lax.dot_general(
        hid_one, grad_two, (((0,), (0,)), ((), ())), preferred_element_type=jnp.float32
    )
    back_one = lax.dot_general(
        grad_two, w_mid, (((1,), (1,)), ((), ())), preferred_element_type=jnp.float32
    )
    grad_one = (back_one * silu_slope(pre_one)).astype(jnp.bfloat16)
    grad_in = lax.dot_general(
        inputs, grad_one, (((0,), (0,)), ((), ())), preferred_element_type=jnp.float32
    )
    rows = grad_in.shape[0] + grad_mid.shape[0] + grad_out.shape[0]
    n_chains = len(chain_orders(levels))
    cut = [(rows * c // n_chains) // 8 * 8 for c in range(n_chains + 1)]
    cut[-1] = rows
    stacked = jnp.concatenate([grad_mid, grad_in, grad_out], axis=0)
    pieces = chained_all_reduce(
        [stacked[cut[c]:cut[c + 1]] for c in range(n_chains)], levels, devices, device_id
    )
    stacked = jnp.concatenate(pieces, axis=0)
    n_mid, n_in = grad_mid.shape[0], grad_in.shape[0]
    grad_mid = stacked[:n_mid]
    grad_in = stacked[n_mid:n_mid + n_in]
    grad_out = stacked[n_mid + n_in:]
    return (solution, grad_in, grad_mid, grad_out)


def solution(mesh):
    in_specs = (P("pts", None), P("pts"), P(), P(), P(), P())
    out_specs = (P("pts"), P(), P(), P())
    return jax.shard_map(
        on_device, mesh=mesh, in_specs=in_specs, out_specs=out_specs, check_vma=False
    )
```

```python
import math

import jax
import jax.numpy as jnp
from jax import lax
from jax.sharding import PartitionSpec as P

ITERS = 2


noise_level = 1.0
highest = lax.Precision.HIGHEST
high = lax.Precision.HIGH


def kernel_block(left_feats, right_feats):
    cross_term = jnp.dot(
        left_feats.T, right_feats, precision=highest, preferred_element_type=jnp.float32
    )
    norm_left = jnp.sum(left_feats * left_feats, axis=0)
    norm_right = jnp.sum(right_feats * right_feats, axis=0)
    return jnp.exp(-0.5 * (norm_left[:, None] + norm_right[None, :] - 2.0 * cross_term))


def silu_slope(pre_act):
    sigmoid_val = jax.nn.sigmoid(pre_act)
    return sigmoid_val * (1.0 + pre_act * (1.0 - sigmoid_val))


def kernel_times(kernel, vec):
    return jnp.sum(kernel * vec[None, :], axis=1)


def project(basis, vec):
    return jnp.sum(basis * vec[None, :, None], axis=1)


def spread(basis, node_vals):
    return jnp.sum(basis * node_vals[:, None, :], axis=(0, 2))


def butterfly(parts, scalars, bits, devices, hook=None, tie=None):
    parts = list(parts)
    for b in range(bits):
        live = [p.reshape(-1) for p in parts[b:]]
        if scalars is not None:
            live.append(scalars)
        payload = jnp.concatenate(live) if len(live) > 1 else live[0]
        recv = lax.ppermute(payload, "pts", [(i, i ^ (1 << b)) for i in range(devices)])
        total = payload + recv
        offset = 0
        for h in range(b, len(parts)):
            size = parts[h].size
            parts[h] = total[offset:offset + size].reshape(parts[h].shape)
            offset += size
        if scalars is not None:
            scalars = total[offset:]
        if hook is not None:
            scalars = hook(b, parts[b], scalars)
        if b == 0 and tie is not None:
            tie = lax.optimization_barrier((tie, parts[0]))[0]
    if tie is not None:
        return parts, scalars, tie
    return parts, scalars


def chain_orders(bits):
    if bits == 7:
        return [(0, 1, 3, 5, 2, 4, 6), (0, 3, 5, 1, 4, 6, 2), (0, 5, 1, 3, 6, 2, 4)]
    return [tuple(range(bits))]


def chained_all_reduce(chunks, bits, devices, device_id):
    orders = chain_orders(bits)
    chunks = list(chunks)
    for rnd in range(bits):
        for c, order in enumerate(orders):
            bit_index = order[rnd]
            half = chunks[c].shape[1] // 2
            upper = jnp.right_shift(device_id, bit_index) & 1
            keep = lax.dynamic_slice_in_dim(chunks[c], upper * half, half, axis=1)
            send = lax.dynamic_slice_in_dim(chunks[c], (1 - upper) * half, half, axis=1)
            chunks[c] = keep + xor_permute(send, bit_index, devices)
    for rnd in reversed(range(bits)):
        for c, order in enumerate(orders):
            bit_index = order[rnd]
            upper = jnp.right_shift(device_id, bit_index) & 1
            other = xor_permute(chunks[c], bit_index, devices)
            low = jnp.where(upper == 0, chunks[c], other)
            high = jnp.where(upper == 0, other, chunks[c])
            chunks[c] = jnp.concatenate([low, high], axis=1)
    return chunks


def xor_permute(x, bit_index, devices):
    return lax.ppermute(x, "pts", [(i, i ^ (1 << bit_index)) for i in range(devices)])


def on_device(inputs, targets, skeletons, w_in, w_mid, w_out):
    devices = lax.axis_size("pts")
    levels = devices.bit_length() - 1
    device_id = lax.axis_index("pts")
    leaf_size = inputs.shape[0]
    skel_width = skeletons.shape[1]
    points = leaf_size * devices
    pre_one = jnp.dot(inputs, w_in, preferred_element_type=jnp.float32)
    hid_one = jax.nn.silu(pre_one).astype(jnp.bfloat16)
    pre_two = jnp.dot(hid_one, w_mid, preferred_element_type=jnp.float32)
    hid_two = jax.nn.silu(pre_two).astype(jnp.bfloat16)
    features = lax.dot_general(
        w_out, hid_two, (((1,), (1,)), ((), ())), preferred_element_type=jnp.float32
    )

    rows = jnp.stack(
        [
            lax.dynamic_index_in_dim(
                skeletons, jnp.right_shift(devices + device_id, height + 1) - 1, 0, False
            )
            for height in range(levels)
        ]
    )
    local_slots = rows - device_id * leaf_size
    route = (local_slots[:, :, None] == jnp.arange(leaf_size)[None, None, :]).astype(jnp.float32)
    pieces = jnp.einsum("fp,lsp->lfs", features, route, precision=highest)

    res_local = jnp.sum(targets * targets)
    skel_parts, scal = butterfly(list(pieces), res_local[None], levels, devices)
    res_norm = scal[0]
    skel_feats = jnp.stack(skel_parts)

    leaf_kernel = kernel_block(features, features)
    basis_maps = jnp.stack([kernel_block(features, skel_feats[h]) for h in range(levels)])

    def node_term(height, part, scalars):
        return scalars + jnp.concatenate(
            [jnp.zeros((1,), jnp.float32), (jnp.sum(part * part) / skel_width)[None]]
        )

    dir0 = targets
    near0 = kernel_times(leaf_kernel, dir0)
    proj0 = project(basis_maps, dir0)
    own0 = jnp.sum(dir0 * (noise_level * dir0 + near0))
    parts0, scal0 = butterfly(
        list(proj0), jnp.stack([own0, jnp.zeros((), jnp.float32)]), levels, devices, node_term
    )
    node0 = jnp.stack(parts0)
    curve0 = scal0[0] + scal0[1]
    step0 = res_norm / curve0
    far0 = spread(basis_maps, node0) / skel_width
    image0 = noise_level * dir0 + near0 + far0
    sol_half = step0 * dir0
    resid = dir0 - step0 * image0

    near_res = kernel_times(leaf_kernel, resid)
    proj_res = project(basis_maps, resid)
    own_res = jnp.stack(
        [
            jnp.sum(resid * resid),
            jnp.sum(resid * (noise_level * resid + near_res)),
            jnp.sum(resid * image0),
            jnp.zeros((), jnp.float32),
        ]
    )

    def node_term_res(height, part, scalars):
        return scalars + jnp.concatenate(
            [jnp.zeros((3,), jnp.float32), (jnp.sum(part * part) / skel_width)[None]]
        )

    parts_r, scal_r = butterfly(list(proj_res), own_res, levels, devices, node_term_res)
    node_res = jnp.stack(parts_r)
    new_norm = scal_r[0]
    beta = new_norm / res_norm
    dir1 = resid + beta * dir0
    node1 = node_res + beta * node0
    curve1 = (scal_r[1] + scal_r[3]) + 2.0 * beta * scal_r[2] + beta * beta * curve0
    step1 = new_norm / curve1
    solution = sol_half + step1 * dir1
    node_sol = step0 * node0 + step1 * node1

    scaled = features * solution[None, :]
    toward = jnp.einsum("fp,lps->lfs", scaled, basis_maps, precision=high)
    proj_sol = project(basis_maps, solution)
    grad_skel = node_sol[:, None, :] * (toward - skel_feats * proj_sol[:, None, :]) / skel_width
    skel_sum, _, (late_sol, late_scaled, late_node) = butterfly(
        list(grad_skel), None, levels, devices, tie=(solution, scaled, node_sol)
    )
    kern_sol = kernel_times(leaf_kernel, late_sol)
    grad_leaf = late_sol[None, :] * (
        jnp.dot(late_scaled, leaf_kernel, precision=high, preferred_element_type=jnp.float32)
        - features * kern_sol[None, :]
    )
    expand = spread(basis_maps, late_node)
    weighted = skel_feats * late_node[:, None, :]
    pulled = jnp.einsum("lfs,lps->fp", weighted, basis_maps, precision=high)
    grad_pts = late_sol[None, :] * (pulled - features * expand[None, :]) / skel_width
    routed = jnp.einsum("lfs,lsp->fp", jnp.stack(skel_sum), route, precision=high)
    feat_grad = (grad_leaf + grad_pts + routed) / math.sqrt(points)

    low_grad = feat_grad.astype(jnp.bfloat16)
    grad_out = jnp.dot(low_grad, hid_two, preferred_element_type=jnp.float32)
    back_two = lax.dot_general(
        low_grad, w_out, (((0,), (0,)), ((), ())), preferred_element_type=jnp.float32
    )
    grad_two = (back_two * silu_slope(pre_two)).astype(jnp.bfloat16)
    grad_mid = lax.dot_general(
        hid_one, grad_two, (((0,), (0,)), ((), ())), preferred_element_type=jnp.float32
    )
    back_one = lax.dot_general(
        grad_two, w_mid, (((1,), (1,)), ((), ())), preferred_element_type=jnp.float32
    )
    grad_one = (back_one * silu_slope(pre_one)).astype(jnp.bfloat16)
    grad_in = lax.dot_general(
        inputs, grad_one, (((0,), (0,)), ((), ())), preferred_element_type=jnp.float32
    )
    rows = grad_in.shape[0] + grad_mid.shape[0] + grad_out.shape[0]
    n_chains = len(chain_orders(levels))
    cut = [(rows * c // n_chains) // 8 * 8 for c in range(n_chains + 1)]
    cut[-1] = rows
    stacked = jnp.concatenate([grad_mid, grad_in, grad_out], axis=0)
    pieces = chained_all_reduce(
        [stacked[cut[c]:cut[c + 1]] for c in range(n_chains)], levels, devices, device_id
    )
    stacked = jnp.concatenate(pieces, axis=0)
    n_mid, n_in = grad_mid.shape[0], grad_in.shape[0]
    grad_mid = stacked[:n_mid]
    grad_in = stacked[n_mid:n_mid + n_in]
    grad_out = stacked[n_mid + n_in:]
    return (solution, grad_in, grad_mid, grad_out)


def solution(mesh):
    in_specs = (P("pts", None), P("pts"), P(), P(), P(), P())
    out_specs = (P("pts"), P(), P(), P())
    return jax.shard_map(
        on_device, mesh=mesh, in_specs=in_specs, out_specs=out_specs, check_vma=False
    )
```

```python
import math

import jax
import jax.numpy as jnp
from jax import lax
from jax.sharding import PartitionSpec as P

ITERS = 2


noise_level = 1.0
highest = lax.Precision.HIGHEST
high = lax.Precision.HIGH


def kernel_block(left_feats, right_feats):
    cross_term = jnp.dot(
        left_feats.T, right_feats, precision=highest, preferred_element_type=jnp.float32
    )
    norm_left = jnp.sum(left_feats * left_feats, axis=0)
    norm_right = jnp.sum(right_feats * right_feats, axis=0)
    return jnp.exp(-0.5 * (norm_left[:, None] + norm_right[None, :] - 2.0 * cross_term))


def silu_slope(pre_act):
    sigmoid_val = jax.nn.sigmoid(pre_act)
    return sigmoid_val * (1.0 + pre_act * (1.0 - sigmoid_val))


def kernel_times(kernel, vec):
    return jnp.sum(kernel * vec[None, :], axis=1)


def project(basis, vec):
    return jnp.sum(basis * vec[None, :, None], axis=1)


def spread(basis, node_vals):
    return jnp.sum(basis * node_vals[:, None, :], axis=(0, 2))


def butterfly(parts, scalars, bits, devices, hook=None, tie=None):
    parts = list(parts)
    for b in range(bits):
        live = [p.reshape(-1) for p in parts[b:]]
        if scalars is not None:
            live.append(scalars)
        payload = jnp.concatenate(live) if len(live) > 1 else live[0]
        recv = lax.ppermute(payload, "pts", [(i, i ^ (1 << b)) for i in range(devices)])
        total = payload + recv
        offset = 0
        for h in range(b, len(parts)):
            size = parts[h].size
            parts[h] = total[offset:offset + size].reshape(parts[h].shape)
            offset += size
        if scalars is not None:
            scalars = total[offset:]
        if hook is not None:
            scalars = hook(b, parts[b], scalars)
        if b == 0 and tie is not None:
            tie = lax.optimization_barrier((tie, parts[0]))[0]
    if tie is not None:
        return parts, scalars, tie
    return parts, scalars


def chain_orders(bits):
    if bits == 7:
        return [(0, 1, 3, 5, 2, 4, 6), (0, 3, 5, 1, 4, 6, 2), (0, 5, 1, 3, 6, 2, 4)]
    return [tuple(range(bits))]


def chained_all_reduce(chunks, bits, devices, device_id):
    orders = chain_orders(bits)
    chunks = list(chunks)
    for rnd in range(bits):
        for c, order in enumerate(orders):
            bit_index = order[rnd]
            half = chunks[c].shape[1] // 2
            upper = jnp.right_shift(device_id, bit_index) & 1
            keep = lax.dynamic_slice_in_dim(chunks[c], upper * half, half, axis=1)
            send = lax.dynamic_slice_in_dim(chunks[c], (1 - upper) * half, half, axis=1)
            chunks[c] = keep + xor_permute(send, bit_index, devices)
    for rnd in reversed(range(bits)):
        for c, order in enumerate(orders):
            bit_index = order[rnd]
            upper = jnp.right_shift(device_id, bit_index) & 1
            other = xor_permute(chunks[c], bit_index, devices)
            low = jnp.where(upper == 0, chunks[c], other)
            high = jnp.where(upper == 0, other, chunks[c])
            chunks[c] = jnp.concatenate([low, high], axis=1)
    return chunks


def xor_permute(x, bit_index, devices):
    return lax.ppermute(x, "pts", [(i, i ^ (1 << bit_index)) for i in range(devices)])


def on_device(inputs, targets, skeletons, w_in, w_mid, w_out):
    devices = lax.axis_size("pts")
    levels = devices.bit_length() - 1
    device_id = lax.axis_index("pts")
    leaf_size = inputs.shape[0]
    skel_width = skeletons.shape[1]
    points = leaf_size * devices
    pre_one = jnp.dot(inputs, w_in, preferred_element_type=jnp.float32)
    hid_one = jax.nn.silu(pre_one).astype(jnp.bfloat16)
    pre_two = jnp.dot(hid_one, w_mid, preferred_element_type=jnp.float32)
    hid_two = jax.nn.silu(pre_two).astype(jnp.bfloat16)
    features = lax.dot_general(
        w_out, hid_two, (((1,), (1,)), ((), ())), preferred_element_type=jnp.float32
    )

    rows = jnp.stack(
        [
            lax.dynamic_index_in_dim(
                skeletons, jnp.right_shift(devices + device_id, height + 1) - 1, 0, False
            )
            for height in range(levels)
        ]
    )
    local_slots = rows - device_id * leaf_size
    route = (local_slots[:, :, None] == jnp.arange(leaf_size)[None, None, :]).astype(jnp.float32)
    pieces = jnp.einsum("fp,lsp->lfs", features, route, precision=highest)

    res_local = jnp.sum(targets * targets)
    skel_parts, scal, (late_feats, late_targets) = butterfly(
        list(pieces), res_local[None], levels, devices, tie=(features, targets)
    )
    res_norm = scal[0]
    skel_feats = jnp.stack(skel_parts)

    leaf_kernel = kernel_block(late_feats, late_feats)
    basis_maps = jnp.stack([kernel_block(features, skel_feats[h]) for h in range(levels)])

    def node_term(height, part, scalars):
        return scalars + jnp.concatenate(
            [jnp.zeros((1,), jnp.float32), (jnp.sum(part * part) / skel_width)[None]]
        )

    dir0 = targets
    near0 = kernel_times(leaf_kernel, late_targets)
    proj0 = project(basis_maps, dir0)
    own0 = jnp.sum(dir0 * (noise_level * dir0 + near0))
    parts0, scal0 = butterfly(
        list(proj0), jnp.stack([own0, jnp.zeros((), jnp.float32)]), levels, devices, node_term
    )
    node0 = jnp.stack(parts0)
    curve0 = scal0[0] + scal0[1]
    step0 = res_norm / curve0
    far0 = spread(basis_maps, node0) / skel_width
    image0 = noise_level * dir0 + near0 + far0
    sol_half = step0 * dir0
    resid = dir0 - step0 * image0

    near_res = kernel_times(leaf_kernel, resid)
    proj_res = project(basis_maps, resid)
    own_res = jnp.stack(
        [
            jnp.sum(resid * resid),
            jnp.sum(resid * (noise_level * resid + near_res)),
            jnp.sum(resid * image0),
            jnp.zeros((), jnp.float32),
        ]
    )

    def node_term_res(height, part, scalars):
        return scalars + jnp.concatenate(
            [jnp.zeros((3,), jnp.float32), (jnp.sum(part * part) / skel_width)[None]]
        )

    parts_r, scal_r = butterfly(list(proj_res), own_res, levels, devices, node_term_res)
    node_res = jnp.stack(parts_r)
    new_norm = scal_r[0]
    beta = new_norm / res_norm
    dir1 = resid + beta * dir0
    node1 = node_res + beta * node0
    curve1 = (scal_r[1] + scal_r[3]) + 2.0 * beta * scal_r[2] + beta * beta * curve0
    step1 = new_norm / curve1
    solution = sol_half + step1 * dir1
    node_sol = step0 * node0 + step1 * node1

    scaled = features * solution[None, :]
    toward = jnp.einsum("fp,lps->lfs", scaled, basis_maps, precision=high)
    proj_sol = project(basis_maps, solution)
    grad_skel = node_sol[:, None, :] * (toward - skel_feats * proj_sol[:, None, :]) / skel_width
    skel_sum, _, (late_sol, late_scaled, late_node) = butterfly(
        list(grad_skel), None, levels, devices, tie=(solution, scaled, node_sol)
    )
    kern_sol = kernel_times(leaf_kernel, late_sol)
    grad_leaf = late_sol[None, :] * (
        jnp.dot(late_scaled, leaf_kernel, precision=high, preferred_element_type=jnp.float32)
        - features * kern_sol[None, :]
    )
    expand = spread(basis_maps, late_node)
    weighted = skel_feats * late_node[:, None, :]
    pulled = jnp.einsum("lfs,lps->fp", weighted, basis_maps, precision=high)
    grad_pts = late_sol[None, :] * (pulled - features * expand[None, :]) / skel_width
    routed = jnp.einsum("lfs,lsp->fp", jnp.stack(skel_sum), route, precision=high)
    feat_grad = (grad_leaf + grad_pts + routed) / math.sqrt(points)

    low_grad = feat_grad.astype(jnp.bfloat16)
    grad_out = jnp.dot(low_grad, hid_two, preferred_element_type=jnp.float32)
    back_two = lax.dot_general(
        low_grad, w_out, (((0,), (0,)), ((), ())), preferred_element_type=jnp.float32
    )
    grad_two = (back_two * silu_slope(pre_two)).astype(jnp.bfloat16)
    grad_mid = lax.dot_general(
        hid_one, grad_two, (((0,), (0,)), ((), ())), preferred_element_type=jnp.float32
    )
    back_one = lax.dot_general(
        grad_two, w_mid, (((1,), (1,)), ((), ())), preferred_element_type=jnp.float32
    )
    grad_one = (back_one * silu_slope(pre_one)).astype(jnp.bfloat16)
    grad_in = lax.dot_general(
        inputs, grad_one, (((0,), (0,)), ((), ())), preferred_element_type=jnp.float32
    )
    rows = grad_in.shape[0] + grad_mid.shape[0] + grad_out.shape[0]
    n_chains = len(chain_orders(levels))
    cut = [(rows * c // n_chains) // 8 * 8 for c in range(n_chains + 1)]
    cut[-1] = rows
    stacked = jnp.concatenate([grad_mid, grad_in, grad_out], axis=0)
    pieces = chained_all_reduce(
        [stacked[cut[c]:cut[c + 1]] for c in range(n_chains)], levels, devices, device_id
    )
    stacked = jnp.concatenate(pieces, axis=0)
    n_mid, n_in = grad_mid.shape[0], grad_in.shape[0]
    grad_mid = stacked[:n_mid]
    grad_in = stacked[n_mid:n_mid + n_in]
    grad_out = stacked[n_mid + n_in:]
    return (solution, grad_in, grad_mid, grad_out)


def solution(mesh):
    in_specs = (P("pts", None), P("pts"), P(), P(), P(), P())
    out_specs = (P("pts"), P(), P(), P())
    return jax.shard_map(
        on_device, mesh=mesh, in_specs=in_specs, out_specs=out_specs, check_vma=False
    )
```

```python
import math

import jax
import jax.numpy as jnp
from jax import lax
from jax.sharding import PartitionSpec as P

ITERS = 2


noise_level = 1.0
highest = lax.Precision.HIGHEST
high = lax.Precision.HIGH


def kernel_block(left_feats, right_feats):
    cross_term = jnp.dot(
        left_feats.T, right_feats, precision=highest, preferred_element_type=jnp.float32
    )
    norm_left = jnp.sum(left_feats * left_feats, axis=0)
    norm_right = jnp.sum(right_feats * right_feats, axis=0)
    return jnp.exp(-0.5 * (norm_left[:, None] + norm_right[None, :] - 2.0 * cross_term))


def silu_slope(pre_act):
    sigmoid_val = jax.nn.sigmoid(pre_act)
    return sigmoid_val * (1.0 + pre_act * (1.0 - sigmoid_val))


def kernel_times(kernel, vec):
    return jnp.sum(kernel * vec[None, :], axis=1)


def project(basis, vec):
    return jnp.sum(basis * vec[None, :, None], axis=1)


def spread(basis, node_vals):
    return jnp.sum(basis * node_vals[:, None, :], axis=(0, 2))


def butterfly(parts, scalars, bits, devices, hook=None, tie=None):
    parts = list(parts)
    for b in range(bits):
        live = [p.reshape(-1) for p in parts[b:]]
        if scalars is not None:
            live.append(scalars)
        payload = jnp.concatenate(live) if len(live) > 1 else live[0]
        recv = lax.ppermute(payload, "pts", [(i, i ^ (1 << b)) for i in range(devices)])
        total = payload + recv
        offset = 0
        for h in range(b, len(parts)):
            size = parts[h].size
            parts[h] = total[offset:offset + size].reshape(parts[h].shape)
            offset += size
        if scalars is not None:
            scalars = total[offset:]
        if hook is not None:
            scalars = hook(b, parts[b], scalars)
        if b == 0 and tie is not None:
            tie = lax.optimization_barrier((tie, parts[0]))[0]
    if tie is not None:
        return parts, scalars, tie
    return parts, scalars


def chain_orders(bits):
    if bits == 7:
        return [(0, 1, 3, 5, 2, 4, 6), (0, 3, 5, 1, 4, 6, 2), (0, 5, 1, 3, 6, 2, 4)]
    return [tuple(range(bits))]


def chained_all_reduce(chunks, bits, devices, device_id):
    orders = chain_orders(bits)
    chunks = list(chunks)
    for rnd in range(bits):
        for c, order in enumerate(orders):
            bit_index = order[rnd]
            half = chunks[c].shape[1] // 2
            upper = jnp.right_shift(device_id, bit_index) & 1
            keep = lax.dynamic_slice_in_dim(chunks[c], upper * half, half, axis=1)
            send = lax.dynamic_slice_in_dim(chunks[c], (1 - upper) * half, half, axis=1)
            chunks[c] = keep + xor_permute(send, bit_index, devices)
    for rnd in reversed(range(bits)):
        for c, order in enumerate(orders):
            bit_index = order[rnd]
            upper = jnp.right_shift(device_id, bit_index) & 1
            other = xor_permute(chunks[c], bit_index, devices)
            low = jnp.where(upper == 0, chunks[c], other)
            high = jnp.where(upper == 0, other, chunks[c])
            chunks[c] = jnp.concatenate([low, high], axis=1)
    return chunks


def xor_permute(x, bit_index, devices):
    return lax.ppermute(x, "pts", [(i, i ^ (1 << bit_index)) for i in range(devices)])


def on_device(inputs, targets, skeletons, w_in, w_mid, w_out):
    devices = lax.axis_size("pts")
    levels = devices.bit_length() - 1
    device_id = lax.axis_index("pts")
    leaf_size = inputs.shape[0]
    skel_width = skeletons.shape[1]
    points = leaf_size * devices
    pre_one = jnp.dot(inputs, w_in, preferred_element_type=jnp.float32)
    hid_one = jax.nn.silu(pre_one).astype(jnp.bfloat16)
    pre_two = jnp.dot(hid_one, w_mid, preferred_element_type=jnp.float32)
    hid_two = jax.nn.silu(pre_two).astype(jnp.bfloat16)
    features = lax.dot_general(
        w_out, hid_two, (((1,), (1,)), ((), ())), preferred_element_type=jnp.float32
    )

    rows = jnp.stack(
        [
            lax.dynamic_index_in_dim(
                skeletons, jnp.right_shift(devices + device_id, height + 1) - 1, 0, False
            )
            for height in range(levels)
        ]
    )
    local_slots = rows - device_id * leaf_size
    route = (local_slots[:, :, None] == jnp.arange(leaf_size)[None, None, :]).astype(jnp.float32)
    pieces = jnp.einsum("fp,lsp->lfs", features, route, precision=high)

    res_local = jnp.sum(targets * targets)
    skel_parts, scal = butterfly(list(pieces), res_local[None], levels, devices)
    res_norm = scal[0]
    skel_feats = jnp.stack(skel_parts)

    leaf_kernel = kernel_block(features, features)
    basis_maps = jnp.stack([kernel_block(features, skel_feats[h]) for h in range(levels)])

    def node_term(height, part, scalars):
        return scalars + jnp.concatenate(
            [jnp.zeros((1,), jnp.float32), (jnp.sum(part * part) / skel_width)[None]]
        )

    dir0 = targets
    near0 = kernel_times(leaf_kernel, dir0)
    proj0 = project(basis_maps, dir0)
    own0 = jnp.sum(dir0 * (noise_level * dir0 + near0))
    parts0, scal0 = butterfly(
        list(proj0), jnp.stack([own0, jnp.zeros((), jnp.float32)]), levels, devices, node_term
    )
    node0 = jnp.stack(parts0)
    curve0 = scal0[0] + scal0[1]
    step0 = res_norm / curve0
    far0 = spread(basis_maps, node0) / skel_width
    image0 = noise_level * dir0 + near0 + far0
    sol_half = step0 * dir0
    resid = dir0 - step0 * image0

    near_res = kernel_times(leaf_kernel, resid)
    proj_res = project(basis_maps, resid)
    own_res = jnp.stack(
        [
            jnp.sum(resid * resid),
            jnp.sum(resid * (noise_level * resid + near_res)),
            jnp.sum(resid * image0),
            jnp.zeros((), jnp.float32),
        ]
    )

    def node_term_res(height, part, scalars):
        return scalars + jnp.concatenate(
            [jnp.zeros((3,), jnp.float32), (jnp.sum(part * part) / skel_width)[None]]
        )

    parts_r, scal_r = butterfly(list(proj_res), own_res, levels, devices, node_term_res)
    node_res = jnp.stack(parts_r)
    new_norm = scal_r[0]
    beta = new_norm / res_norm
    dir1 = resid + beta * dir0
    node1 = node_res + beta * node0
    curve1 = (scal_r[1] + scal_r[3]) + 2.0 * beta * scal_r[2] + beta * beta * curve0
    step1 = new_norm / curve1
    solution = sol_half + step1 * dir1
    node_sol = step0 * node0 + step1 * node1

    scaled = features * solution[None, :]
    toward = jnp.einsum("fp,lps->lfs", scaled, basis_maps, precision=high)
    proj_sol = project(basis_maps, solution)
    grad_skel = node_sol[:, None, :] * (toward - skel_feats * proj_sol[:, None, :]) / skel_width
    skel_sum, _, (late_sol, late_scaled, late_node) = butterfly(
        list(grad_skel), None, levels, devices, tie=(solution, scaled, node_sol)
    )
    kern_sol = kernel_times(leaf_kernel, late_sol)
    grad_leaf = late_sol[None, :] * (
        jnp.dot(late_scaled, leaf_kernel, precision=high, preferred_element_type=jnp.float32)
        - features * kern_sol[None, :]
    )
    expand = spread(basis_maps, late_node)
    weighted = skel_feats * late_node[:, None, :]
    pulled = jnp.einsum("lfs,lps->fp", weighted, basis_maps, precision=high)
    grad_pts = late_sol[None, :] * (pulled - features * expand[None, :]) / skel_width
    routed = jnp.einsum("lfs,lsp->fp", jnp.stack(skel_sum), route, precision=high)
    feat_grad = (grad_leaf + grad_pts + routed) / math.sqrt(points)

    low_grad = feat_grad.astype(jnp.bfloat16)
    grad_out = jnp.dot(low_grad, hid_two, preferred_element_type=jnp.float32)
    back_two = lax.dot_general(
        low_grad, w_out, (((0,), (0,)), ((), ())), preferred_element_type=jnp.float32
    )
    grad_two = (back_two * silu_slope(pre_two)).astype(jnp.bfloat16)
    grad_mid = lax.dot_general(
        hid_one, grad_two, (((0,), (0,)), ((), ())), preferred_element_type=jnp.float32
    )
    back_one = lax.dot_general(
        grad_two, w_mid, (((1,), (1,)), ((), ())), preferred_element_type=jnp.float32
    )
    grad_one = (back_one * silu_slope(pre_one)).astype(jnp.bfloat16)
    grad_in = lax.dot_general(
        inputs, grad_one, (((0,), (0,)), ((), ())), preferred_element_type=jnp.float32
    )
    rows = grad_in.shape[0] + grad_mid.shape[0] + grad_out.shape[0]
    n_chains = len(chain_orders(levels))
    cut = [(rows * c // n_chains) // 8 * 8 for c in range(n_chains + 1)]
    cut[-1] = rows
    stacked = jnp.concatenate([grad_mid, grad_in, grad_out], axis=0)
    pieces = chained_all_reduce(
        [stacked[cut[c]:cut[c + 1]] for c in range(n_chains)], levels, devices, device_id
    )
    stacked = jnp.concatenate(pieces, axis=0)
    n_mid, n_in = grad_mid.shape[0], grad_in.shape[0]
    grad_mid = stacked[:n_mid]
    grad_in = stacked[n_mid:n_mid + n_in]
    grad_out = stacked[n_mid + n_in:]
    return (solution, grad_in, grad_mid, grad_out)


def solution(mesh):
    in_specs = (P("pts", None), P("pts"), P(), P(), P(), P())
    out_specs = (P("pts"), P(), P(), P())
    return jax.shard_map(
        on_device, mesh=mesh, in_specs=in_specs, out_specs=out_specs, check_vma=False
    )
```

```python
import math

import jax
import jax.numpy as jnp
from jax import lax
from jax.sharding import PartitionSpec as P

ITERS = 2


noise_level = 1.0
highest = lax.Precision.HIGHEST
high = lax.Precision.HIGH


def kernel_block(left_feats, right_feats):
    cross_term = jnp.dot(
        left_feats.T, right_feats, precision=lax.Precision.HIGH, preferred_element_type=jnp.float32
    )
    norm_left = jnp.sum(left_feats * left_feats, axis=0)
    norm_right = jnp.sum(right_feats * right_feats, axis=0)
    return jnp.exp(-0.5 * (norm_left[:, None] + norm_right[None, :] - 2.0 * cross_term))


def silu_slope(pre_act):
    sigmoid_val = jax.nn.sigmoid(pre_act)
    return sigmoid_val * (1.0 + pre_act * (1.0 - sigmoid_val))


def kernel_times(kernel, vec):
    return jnp.sum(kernel * vec[None, :], axis=1)


def project(basis, vec):
    return jnp.sum(basis * vec[None, :, None], axis=1)


def spread(basis, node_vals):
    return jnp.sum(basis * node_vals[:, None, :], axis=(0, 2))


def butterfly(parts, scalars, bits, devices, hook=None, tie=None):
    parts = list(parts)
    for b in range(bits):
        live = [p.reshape(-1) for p in parts[b:]]
        if scalars is not None:
            live.append(scalars)
        payload = jnp.concatenate(live) if len(live) > 1 else live[0]
        recv = lax.ppermute(payload, "pts", [(i, i ^ (1 << b)) for i in range(devices)])
        total = payload + recv
        offset = 0
        for h in range(b, len(parts)):
            size = parts[h].size
            parts[h] = total[offset:offset + size].reshape(parts[h].shape)
            offset += size
        if scalars is not None:
            scalars = total[offset:]
        if hook is not None:
            scalars = hook(b, parts[b], scalars)
        if b == 0 and tie is not None:
            tie = lax.optimization_barrier((tie, parts[0]))[0]
    if tie is not None:
        return parts, scalars, tie
    return parts, scalars


def chain_orders(bits):
    if bits == 7:
        return [(0, 1, 3, 5, 2, 4, 6), (0, 3, 5, 1, 4, 6, 2), (0, 5, 1, 3, 6, 2, 4)]
    return [tuple(range(bits))]


def chained_all_reduce(chunks, bits, devices, device_id):
    orders = chain_orders(bits)
    chunks = list(chunks)
    for rnd in range(bits):
        for c, order in enumerate(orders):
            bit_index = order[rnd]
            half = chunks[c].shape[1] // 2
            upper = jnp.right_shift(device_id, bit_index) & 1
            keep = lax.dynamic_slice_in_dim(chunks[c], upper * half, half, axis=1)
            send = lax.dynamic_slice_in_dim(chunks[c], (1 - upper) * half, half, axis=1)
            chunks[c] = keep + xor_permute(send, bit_index, devices)
    for rnd in reversed(range(bits)):
        for c, order in enumerate(orders):
            bit_index = order[rnd]
            upper = jnp.right_shift(device_id, bit_index) & 1
            other = xor_permute(chunks[c], bit_index, devices)
            low = jnp.where(upper == 0, chunks[c], other)
            high = jnp.where(upper == 0, other, chunks[c])
            chunks[c] = jnp.concatenate([low, high], axis=1)
    return chunks


def xor_permute(x, bit_index, devices):
    return lax.ppermute(x, "pts", [(i, i ^ (1 << bit_index)) for i in range(devices)])


def on_device(inputs, targets, skeletons, w_in, w_mid, w_out):
    devices = lax.axis_size("pts")
    levels = devices.bit_length() - 1
    device_id = lax.axis_index("pts")
    leaf_size = inputs.shape[0]
    skel_width = skeletons.shape[1]
    points = leaf_size * devices
    pre_one = jnp.dot(inputs, w_in, preferred_element_type=jnp.float32)
    hid_one = jax.nn.silu(pre_one).astype(jnp.bfloat16)
    pre_two = jnp.dot(hid_one, w_mid, preferred_element_type=jnp.float32)
    hid_two = jax.nn.silu(pre_two).astype(jnp.bfloat16)
    features = lax.dot_general(
        w_out, hid_two, (((1,), (1,)), ((), ())), preferred_element_type=jnp.float32
    )

    rows = jnp.stack(
        [
            lax.dynamic_index_in_dim(
                skeletons, jnp.right_shift(devices + device_id, height + 1) - 1, 0, False
            )
            for height in range(levels)
        ]
    )
    local_slots = rows - device_id * leaf_size
    route = (local_slots[:, :, None] == jnp.arange(leaf_size)[None, None, :]).astype(jnp.float32)
    pieces = jnp.einsum("fp,lsp->lfs", features, route, precision=high)

    res_local = jnp.sum(targets * targets)
    skel_parts, scal = butterfly(list(pieces), res_local[None], levels, devices)
    res_norm = scal[0]
    skel_feats = jnp.stack(skel_parts)

    leaf_kernel = kernel_block(features, features)
    basis_maps = jnp.stack([kernel_block(features, skel_feats[h]) for h in range(levels)])

    def node_term(height, part, scalars):
        return scalars + jnp.concatenate(
            [jnp.zeros((1,), jnp.float32), (jnp.sum(part * part) / skel_width)[None]]
        )

    dir0 = targets
    near0 = kernel_times(leaf_kernel, dir0)
    proj0 = project(basis_maps, dir0)
    own0 = jnp.sum(dir0 * (noise_level * dir0 + near0))
    parts0, scal0 = butterfly(
        list(proj0), jnp.stack([own0, jnp.zeros((), jnp.float32)]), levels, devices, node_term
    )
    node0 = jnp.stack(parts0)
    curve0 = scal0[0] + scal0[1]
    step0 = res_norm / curve0
    far0 = spread(basis_maps, node0) / skel_width
    image0 = noise_level * dir0 + near0 + far0
    sol_half = step0 * dir0
    resid = dir0 - step0 * image0

    near_res = kernel_times(leaf_kernel, resid)
    proj_res = project(basis_maps, resid)
    own_res = jnp.stack(
        [
            jnp.sum(resid * resid),
            jnp.sum(resid * (noise_level * resid + near_res)),
            jnp.sum(resid * image0),
            jnp.zeros((), jnp.float32),
        ]
    )

    def node_term_res(height, part, scalars):
        return scalars + jnp.concatenate(
            [jnp.zeros((3,), jnp.float32), (jnp.sum(part * part) / skel_width)[None]]
        )

    parts_r, scal_r = butterfly(list(proj_res), own_res, levels, devices, node_term_res)
    node_res = jnp.stack(parts_r)
    new_norm = scal_r[0]
    beta = new_norm / res_norm
    dir1 = resid + beta * dir0
    node1 = node_res + beta * node0
    curve1 = (scal_r[1] + scal_r[3]) + 2.0 * beta * scal_r[2] + beta * beta * curve0
    step1 = new_norm / curve1
    solution = sol_half + step1 * dir1
    node_sol = step0 * node0 + step1 * node1

    scaled = features * solution[None, :]
    toward = jnp.einsum("fp,lps->lfs", scaled, basis_maps, precision=high)
    proj_sol = project(basis_maps, solution)
    grad_skel = node_sol[:, None, :] * (toward - skel_feats * proj_sol[:, None, :]) / skel_width
    skel_sum, _, (late_sol, late_scaled, late_node) = butterfly(
        list(grad_skel), None, levels, devices, tie=(solution, scaled, node_sol)
    )
    kern_sol = kernel_times(leaf_kernel, late_sol)
    grad_leaf = late_sol[None, :] * (
        jnp.dot(late_scaled, leaf_kernel, precision=high, preferred_element_type=jnp.float32)
        - features * kern_sol[None, :]
    )
    expand = spread(basis_maps, late_node)
    weighted = skel_feats * late_node[:, None, :]
    pulled = jnp.einsum("lfs,lps->fp", weighted, basis_maps, precision=high)
    grad_pts = late_sol[None, :] * (pulled - features * expand[None, :]) / skel_width
    routed = jnp.einsum("lfs,lsp->fp", jnp.stack(skel_sum), route, precision=high)
    feat_grad = (grad_leaf + grad_pts + routed) / math.sqrt(points)

    low_grad = feat_grad.astype(jnp.bfloat16)
    grad_out = jnp.dot(low_grad, hid_two, preferred_element_type=jnp.float32)
    back_two = lax.dot_general(
        low_grad, w_out, (((0,), (0,)), ((), ())), preferred_element_type=jnp.float32
    )
    grad_two = (back_two * silu_slope(pre_two)).astype(jnp.bfloat16)
    grad_mid = lax.dot_general(
        hid_one, grad_two, (((0,), (0,)), ((), ())), preferred_element_type=jnp.float32
    )
    back_one = lax.dot_general(
        grad_two, w_mid, (((1,), (1,)), ((), ())), preferred_element_type=jnp.float32
    )
    grad_one = (back_one * silu_slope(pre_one)).astype(jnp.bfloat16)
    grad_in = lax.dot_general(
        inputs, grad_one, (((0,), (0,)), ((), ())), preferred_element_type=jnp.float32
    )
    rows = grad_in.shape[0] + grad_mid.shape[0] + grad_out.shape[0]
    n_chains = len(chain_orders(levels))
    cut = [(rows * c // n_chains) // 8 * 8 for c in range(n_chains + 1)]
    cut[-1] = rows
    stacked = jnp.concatenate([grad_mid, grad_in, grad_out], axis=0)
    pieces = chained_all_reduce(
        [stacked[cut[c]:cut[c + 1]] for c in range(n_chains)], levels, devices, device_id
    )
    stacked = jnp.concatenate(pieces, axis=0)
    n_mid, n_in = grad_mid.shape[0], grad_in.shape[0]
    grad_mid = stacked[:n_mid]
    grad_in = stacked[n_mid:n_mid + n_in]
    grad_out = stacked[n_mid + n_in:]
    return (solution, grad_in, grad_mid, grad_out)


def solution(mesh):
    in_specs = (P("pts", None), P("pts"), P(), P(), P(), P())
    out_specs = (P("pts"), P(), P(), P())
    return jax.shard_map(
        on_device, mesh=mesh, in_specs=in_specs, out_specs=out_specs, check_vma=False
    )
```
